256 devices in a mesh: gx: 16 (over z, core), gy: 16 (over y, x).
Axes of the slice: x: 4, y: 4, z: 8, core: 2. Of those that a mesh axis runs over, the one named last changes fastest.
Arguments:
- right_side: float32 [256, 128, 1024], P('gx', 'gy'), may hold values from -340 to 340
- start_guess: float32 [256, 128, 1024], P('gx', 'gy'), may hold values from -1.8 to 1.8
- couple_x: float32 [256, 128, 64], P('gx', 'gy'), may hold values from 0.3 to 3
- couple_y: float32 [256, 128, 64], P('gx', 'gy'), may hold values from 0.3 to 3
- couple_z: float32 [256, 128, 64], P('gx', 'gy'), may hold values from 0.3 to 3
- reaction: float32 [256, 128, 64], P('gx', 'gy'), may hold values from 0.01 to 0.1
Outputs:
- solution: float32 [256, 128, 1024], P('gx', 'gy')
- residual: float32 [256, 128, 1024], P('gx', 'gy')
The draws below stay inside these ranges and needn't reach their ends.
All inputs are finite; a program needn't handle non-finite values.
Results may differ from the reference program's by a relative error of at most 0.0003.
Values sent between devices are 32-bit elements; how exact they have to be, the bound alone decides.
No kernel may reach another device: no remote copies, remote signals or barrier semaphores. Data moves between devices by JAX's collectives and lax.ppermute only.
A program may use at most 64 MiB of HBM per device.

```python
import math
import jax
import jax.numpy as jnp
from jax import lax

CX = 16
CY = 8
NZ = 64
S = 16
ITERS = 2
SWEEPS = 4
FACT_SWEEPS = 3
NX = 256
NY = 128


def draw_right_side(key, part):
    key_base = jax.random.fold_in(jax.random.fold_in(key, 11), 0)
    pos_x = jnp.arange(NX, dtype=jnp.float32)[:, None, None]
    pos_y = jnp.arange(NY, dtype=jnp.float32)[None, :, None]
    rising = jnp.exp(math.log(3.0) * pos_x / max(NX - 1, 1)) * jnp.exp(math.log(3.0) * pos_y / max(NY - 1, 1))
    base = jnp.clip(jax.random.normal(key_base, (NX, NY, S * NZ), jnp.float32), -4.0, 4.0)
    return (2.0 * base * rising).astype(jnp.float32)


def level_of(key, dims, pieces, least, top_value):
    def one(dim, blocks):
        heights = jax.random.uniform(jax.random.fold_in(jax.random.fold_in(key, 6), dim), (blocks,), jnp.float32, least / len(pieces), top_value / len(pieces))
        return jnp.repeat(jnp.exp(heights), dims[dim] // blocks).reshape((-1,) + (1,) * (len(dims) - dim - 1))

    level = one(*pieces[0])
    for cut in pieces[1:]:
        level = level * one(*cut)
    return level


def bell_draw(own_key, dims, spread, limit, cuts=(), held_as=jnp.bfloat16):
    factor_of = level_of(own_key, dims, cuts, -0.22, 0.18) if cuts else 1.0
    drawn = jax.random.normal(own_key, dims, jnp.float32) * spread * factor_of
    return jnp.minimum(jnp.maximum(drawn, -limit), limit).astype(held_as)


def setup_inputs(seed: int = 0) -> dict:
    keys = jax.random.split(jax.random.key(seed), 7)
    return {
        "right_side": draw_right_side(jax.random.fold_in(keys[6], 71), 0),
        "start_guess": bell_draw(keys[1], (NX, NY, S * NZ), 0.3, 1.8, ((0, 16), (1, 16)), jnp.float32),
        "couple_x": jnp.clip(jnp.exp(math.log(3.0) - 2.3025851 * jax.random.uniform(keys[2], (NX, NY, NZ), jnp.float32) ** level_of(keys[2], (NX, NY, NZ), ((0, 16), (1, 16)), -0.2, 0.2)), 0.3, 3.0),
        "couple_y": jnp.clip(jnp.exp(math.log(3.0) - 2.3025851 * jax.random.uniform(keys[3], (NX, NY, NZ), jnp.float32) ** level_of(keys[3], (NX, NY, NZ), ((0, 16), (1, 16)), -0.2, 0.2)), 0.3, 3.0),
        "couple_z": jnp.clip(jnp.exp(math.log(3.0) - 2.3025851 * jax.random.uniform(keys[4], (NX, NY, NZ), jnp.float32) ** level_of(keys[4], (NX, NY, NZ), ((0, 16), (1, 16)), -0.2, 0.2)), 0.3, 3.0),
        "reaction": jnp.clip(jnp.exp(math.log(0.1) - 2.3025851 * jax.random.uniform(keys[5], (NX, NY, NZ), jnp.float32) ** level_of(keys[5], (NX, NY, NZ), ((0, 16), (1, 16)), -0.2, 0.2)), 0.01, 0.1),
    }


HIGH = lax.Precision.HIGHEST

def low_shift(values, along):
    count = values.shape[along]
    blank = jnp.zeros_like(lax.slice_in_dim(values, 0, 1, axis=along))
    return jnp.concatenate([blank, lax.slice_in_dim(values, 0, count - 1, axis=along)], axis=along)

def up_shift(values, along):
    count = values.shape[along]
    blank = jnp.zeros_like(lax.slice_in_dim(values, 0, 1, axis=along))
    return jnp.concatenate([lax.slice_in_dim(values, 1, count, axis=along), blank], axis=along)

def block_gram(former, latter):
    return jnp.einsum('xysz,xytz->st', former, latter, precision=HIGH)

def mix_block(values, matrix):
    return jnp.einsum('xysz,st->xytz', values, matrix, precision=HIGH)

def chol_factor(gram_mat):
    low_factor = jnp.linalg.cholesky(gram_mat)
    eye_mat = jnp.eye(gram_mat.shape[0], dtype=gram_mat.dtype)
    inverse = lax.linalg.triangular_solve(low_factor, eye_mat, left_side=True, lower=True)
    return (low_factor.T, inverse.T)

def pivot_setup(diagonal, lows):
    pivots = diagonal
    for repeat in range(FACT_SWEEPS):
        inv_piv = 1.0 / pivots
        pivots = diagonal - lows[0] * lows[0] * low_shift(inv_piv, 0) - lows[1] * lows[1] * low_shift(inv_piv, 1) - lows[2] * lows[2] * low_shift(inv_piv, 3)
    return 1.0 / pivots

def precondition(source, inv_piv, lows, ups):
    lower_sol = inv_piv * source
    for repeat in range(SWEEPS):
        lower_sol = inv_piv * (source + lows[0] * low_shift(lower_sol, 0) + lows[1] * low_shift(lower_sol, 1) + lows[2] * low_shift(lower_sol, 3))
    upper_sol = lower_sol
    for repeat in range(SWEEPS):
        upper_sol = lower_sol + inv_piv * (ups[0] * up_shift(upper_sol, 0) + ups[1] * up_shift(upper_sol, 1) + ups[2] * up_shift(upper_sol, 3))
    return upper_sol

def solve_small(columns, first_factor):
    hessen = jnp.concatenate(columns, axis=1)
    count_rhs = first_factor.shape[0]
    target = jnp.dot(hessen[:count_rhs].T, first_factor, precision=HIGH)
    normal = jnp.dot(hessen.T, hessen, precision=HIGH)
    low_factor = jnp.linalg.cholesky(normal)
    partial_sol = lax.linalg.triangular_solve(low_factor, target, left_side=True, lower=True)
    return lax.linalg.triangular_solve(low_factor, partial_sol, left_side=True, lower=True, transpose_a=True)

def reference(right_side, start_guess, couple_x, couple_y, couple_z, reaction):
    rhs_block = right_side.reshape(NX, NY, S, NZ)
    start_block = start_guess.reshape(NX, NY, S, NZ)
    after_x = couple_x[:, :, None, :]
    after_y = couple_y[:, :, None, :]
    after_z = couple_z[:, :, None, :]
    before_x = low_shift(after_x, 0)
    before_y = low_shift(after_y, 1)
    before_z = low_shift(after_z, 3)
    diagonal = reaction[:, :, None, :] + after_x + before_x + after_y + before_y + after_z + before_z

    def apply_op(values):
        return diagonal * values - after_x * up_shift(values, 0) - before_x * low_shift(values, 0) - after_y * up_shift(values, 1) - before_y * low_shift(values, 1) - after_z * up_shift(values, 3) - before_z * low_shift(values, 3)
    index_x = jnp.arange(NX, dtype=jnp.int32)
    index_y = jnp.arange(NY, dtype=jnp.int32)
    lowmask_x = (index_x % CX != 0).astype(jnp.float32)[:, None, None, None]
    lowmask_y = (index_y % CY != 0).astype(jnp.float32)[None, :, None, None]
    upmask_x = (index_x % CX != CX - 1).astype(jnp.float32)[:, None, None, None]
    upmask_y = (index_y % CY != CY - 1).astype(jnp.float32)[None, :, None, None]
    lows = (before_x * lowmask_x, before_y * lowmask_y, before_z)
    ups = (after_x * upmask_x, after_y * upmask_y, after_z)
    inv_piv = pivot_setup(diagonal, lows)
    start_res = rhs_block - apply_op(start_block)
    first_factor, first_inv = chol_factor(block_gram(start_res, start_res))
    basis_set = [mix_block(start_res, first_inv)]
    precond_set = []
    columns = []
    for column in range(ITERS):
        precond_blk = precondition(basis_set[column], inv_piv, lows, ups)
        image = apply_op(precond_blk)
        precond_set.append(precond_blk)
        projections = [block_gram(member, image) for member in basis_set]
        removed = mix_block(basis_set[0], projections[0])
        for member in range(1, len(basis_set)):
            removed = removed + mix_block(basis_set[member], projections[member])
        perp = image - removed
        next_factor, next_inv = chol_factor(block_gram(perp, perp))
        if column + 1 < ITERS:
            basis_set.append(mix_block(perp, next_inv))
        blank = jnp.zeros(((ITERS - 1 - column) * S, S), dtype=next_factor.dtype)
        columns.append(jnp.concatenate(projections + [next_factor, blank], axis=0))
    coeffs = solve_small(columns, first_factor)
    solution = start_block
    for column in range(ITERS):
        solution = solution + mix_block(precond_set[column], coeffs[column * S:(column + 1) * S])
    residual = rhs_block - apply_op(solution)
    return (solution.reshape(NX, NY, S * NZ), residual.reshape(NX, NY, S * NZ))
```

```python
import jax
import jax.numpy as jnp
from jax import lax
from jax.sharding import PartitionSpec as P

ITERS = 2
SWEEPS = 4
FACT_SWEEPS = 3


HIGH = lax.Precision.HIGHEST


def passed_along(block, axis, distance):
    devices = range(lax.axis_size(axis))
    route = [(i - distance, i) for i in devices if i - distance in devices]
    return lax.ppermute(block, axis, route)


def mesh_sum(block):
    for axis in ("gx", "gy"):
        count = lax.axis_size(axis)
        if count & (count - 1):
            block = lax.psum(block, axis)
            continue
        step = 1
        while step < count:
            radix = 4 if count % (step * 4) == 0 else 2
            parts = [block] + [
                lax.ppermute(block, axis, [(i, i ^ (step * m)) for i in range(count)])
                for m in range(1, radix)
            ]
            while len(parts) > 1:
                parts = [parts[i] + parts[i + 1] for i in range(0, len(parts), 2)]
            block = parts[0]
            step *= radix
    return block


def padded_2(block, sides, width):
    for axis, dim in sides:
        count = lax.axis_size(axis)
        forward = [(i, i + 1) for i in range(count - 1)]
        backward = [(target, source) for source, target in forward]
        low = lax.ppermute(
            lax.slice_in_dim(block, block.shape[dim] - width, None, axis=dim), axis, forward
        )
        high = lax.ppermute(lax.slice_in_dim(block, 0, width, axis=dim), axis, backward)
        block = jnp.concatenate([low, block, high], axis=dim)
    return block


def low_shift(values, along):
    count = values.shape[along]
    blank = jnp.zeros_like(lax.slice_in_dim(values, 0, 1, axis=along))
    return jnp.concatenate([blank, lax.slice_in_dim(values, 0, count - 1, axis=along)], axis=along)


def up_shift(values, along):
    count = values.shape[along]
    blank = jnp.zeros_like(lax.slice_in_dim(values, 0, 1, axis=along))
    return jnp.concatenate([lax.slice_in_dim(values, 1, count, axis=along), blank], axis=along)


def block_gram(former, latter, count_rhs):
    cells = former.shape[0] * former.shape[1]
    left = former.reshape(cells, count_rhs, -1)
    right = latter.reshape(cells, count_rhs, -1)
    return jnp.einsum("psz,ptz->st", left, right, precision=HIGH)


def mix_block(values, matrix):
    rows_x, rows_y, flat_len = values.shape
    count_rhs = matrix.shape[0]
    split = values.reshape(rows_x * rows_y, count_rhs, flat_len // count_rhs)
    return jnp.einsum("psz,st->ptz", split, matrix, precision=HIGH).reshape(
        rows_x, rows_y, flat_len
    )


def chol_factor(gram_mat):
    low_factor = jnp.linalg.cholesky(gram_mat)
    eye_mat = jnp.eye(gram_mat.shape[0], dtype=gram_mat.dtype)
    inverse = lax.linalg.triangular_solve(low_factor, eye_mat, left_side=True, lower=True)
    return (low_factor.T, inverse.T)


def solve_small(columns, first_factor):
    hessen = jnp.concatenate(columns, axis=1)
    count_rhs = first_factor.shape[0]
    target = jnp.dot(hessen[:count_rhs].T, first_factor, precision=HIGH)
    normal = jnp.dot(hessen.T, hessen, precision=HIGH)
    low_factor = jnp.linalg.cholesky(normal)
    partial_sol = lax.linalg.triangular_solve(low_factor, target, left_side=True, lower=True)
    return lax.linalg.triangular_solve(
        low_factor, partial_sol, left_side=True, lower=True, transpose_a=True
    )


def body(right_side, start_guess, couple_x, couple_y, couple_z, reaction):
    rows_x, rows_y, flat_len = right_side.shape
    layers = couple_z.shape[2]
    count_rhs = flat_len // layers
    depth = jnp.arange(flat_len, dtype=jnp.int32) % layers
    keep_first = (depth != 0).astype(jnp.float32)
    keep_last = (depth != layers - 1).astype(jnp.float32)

    def low_z(values):
        return low_shift(values, 2) * keep_first

    def up_z(values):
        return up_shift(values, 2) * keep_last

    def tiled(values):
        return jnp.tile(values, (1, 1, count_rhs))

    edge_x = passed_along(couple_x[-1:], "gx", 1)
    edge_y = passed_along(couple_y[:, -1:], "gy", 1)
    after_x = tiled(couple_x)
    after_y = tiled(couple_y)
    after_z = tiled(couple_z)
    before_x = tiled(jnp.concatenate([edge_x, couple_x[:-1]], axis=0))
    before_y = tiled(jnp.concatenate([edge_y, couple_y[:, :-1]], axis=1))
    before_z = low_z(after_z)
    diagonal = tiled(reaction) + after_x + before_x + after_y + before_y + after_z + before_z

    def apply_op(values):
        padded = padded_2(values, (("gx", 0), ("gy", 1)), 1)
        centre = padded[1:-1, 1:-1]
        return (
            diagonal * centre
            - after_x * padded[2:, 1:-1]
            - before_x * padded[:-2, 1:-1]
            - after_y * padded[1:-1, 2:]
            - before_y * padded[1:-1, :-2]
            - after_z * up_z(centre)
            - before_z * low_z(centre)
        )

    lows = (low_shift(after_x, 0), low_shift(after_y, 1), before_z)
    ups = (
        up_shift(jnp.ones_like(after_x), 0) * after_x,
        up_shift(jnp.ones_like(after_y), 1) * after_y,
        after_z,
    )
    pivots = diagonal
    for repeat in range(FACT_SWEEPS):
        inv_now = 1.0 / pivots
        pivots = (
            diagonal
            - lows[0] * lows[0] * low_shift(inv_now, 0)
            - lows[1] * lows[1] * low_shift(inv_now, 1)
            - lows[2] * lows[2] * low_z(inv_now)
        )
    inv_piv = 1.0 / pivots

    def total_gram(former, latter):
        return mesh_sum(block_gram(former, latter, count_rhs))

    start_res = right_side - apply_op(start_guess)
    first_factor, first_inv = chol_factor(total_gram(start_res, start_res))
    basis_set = [mix_block(start_res, first_inv)]
    precond_set = []
    image_set = []
    columns = []
    for column in range(ITERS):
        source = basis_set[column]
        lower_sol = inv_piv * source
        for precondition_repeat in range(SWEEPS):
            lower_sol = inv_piv * (
                source
                + lows[0] * low_shift(lower_sol, 0)
                + lows[1] * low_shift(lower_sol, 1)
                + lows[2] * low_z(lower_sol)
            )
        upper_sol = lower_sol
        for precondition_repeat in range(SWEEPS):
            upper_sol = lower_sol + inv_piv * (
                ups[0] * up_shift(upper_sol, 0)
                + ups[1] * up_shift(upper_sol, 1)
                + ups[2] * up_z(upper_sol)
            )
        image = apply_op(upper_sol)
        precond_set.append(upper_sol)
        image_set.append(image)
        local_proj = jnp.stack([block_gram(member, image, count_rhs) for member in basis_set])
        stacked = mesh_sum(local_proj)
        projections = [stacked[member] for member in range(len(basis_set))]
        removed = mix_block(basis_set[0], projections[0])
        for member in range(1, len(basis_set)):
            removed = removed + mix_block(basis_set[member], projections[member])
        perp = image - removed
        next_factor, next_inv = chol_factor(total_gram(perp, perp))
        if column + 1 < ITERS:
            basis_set.append(mix_block(perp, next_inv))
        blank = jnp.zeros(((ITERS - 1 - column) * count_rhs, count_rhs), dtype=next_factor.dtype)
        columns.append(jnp.concatenate(projections + [next_factor, blank], axis=0))
    coeffs = solve_small(columns, first_factor)
    solution = start_guess
    for column in range(ITERS):
        solution = solution + mix_block(
            precond_set[column], coeffs[column * count_rhs : (column + 1) * count_rhs]
        )
    residual = right_side - apply_op(solution)
    return (solution, residual)


def solution(mesh):
    return jax.shard_map(
        body,
        mesh=mesh,
        in_specs=(
            P("gx", "gy", None),
            P("gx", "gy", None),
            P("gx", "gy", None),
            P("gx", "gy", None),
            P("gx", "gy", None),
            P("gx", "gy", None),
        ),
        out_specs=(P("gx", "gy", None), P("gx", "gy", None)),
        check_vma=False,
    )
```

```python
import jax
import jax.numpy as jnp
from jax import lax
from jax.sharding import PartitionSpec as P

ITERS = 2
SWEEPS = 4
FACT_SWEEPS = 3


HIGH = lax.Precision.HIGHEST


def mesh_sum(block):
    for axis in ("gx", "gy"):
        count = lax.axis_size(axis)
        if count & (count - 1):
            block = lax.psum(block, axis)
            continue
        step = 1
        while step < count:
            radix = 4 if count % (step * 4) == 0 else 2
            parts = [block] + [
                lax.ppermute(block, axis, [(i, i ^ (step * m)) for i in range(count)])
                for m in range(1, radix)
            ]
            while len(parts) > 1:
                parts = [parts[i] + parts[i + 1] for i in range(0, len(parts), 2)]
            block = parts[0]
            step *= radix
    return block


def low_along(values, axis, width):
    count = values.shape[axis]
    blank = jnp.zeros_like(lax.slice_in_dim(values, 0, width, axis=axis))
    return jnp.concatenate([blank, lax.slice_in_dim(values, 0, count - width, axis=axis)], axis=axis)


def up_along(values, axis, width):
    count = values.shape[axis]
    blank = jnp.zeros_like(lax.slice_in_dim(values, 0, width, axis=axis))
    return jnp.concatenate([lax.slice_in_dim(values, width, count, axis=axis), blank], axis=axis)


def block_gram(former, latter):
    return jnp.einsum("sxl,txl->st", former, latter, precision=HIGH)


def mix_block(values, matrix):
    return jnp.einsum("ts,sxl->txl", matrix.T, values, precision=HIGH)


def chol_factor(gram_mat):
    low_factor = jnp.linalg.cholesky(gram_mat)
    eye_mat = jnp.eye(gram_mat.shape[0], dtype=gram_mat.dtype)
    inverse = lax.linalg.triangular_solve(low_factor, eye_mat, left_side=True, lower=True)
    return (low_factor.T, inverse.T)


def solve_small(columns, first_factor):
    hessen = jnp.concatenate(columns, axis=1)
    count_rhs = first_factor.shape[0]
    target = jnp.dot(hessen[:count_rhs].T, first_factor, precision=HIGH)
    normal = jnp.dot(hessen.T, hessen, precision=HIGH)
    low_factor = jnp.linalg.cholesky(normal)
    partial_sol = lax.linalg.triangular_solve(low_factor, target, left_side=True, lower=True)
    return lax.linalg.triangular_solve(
        low_factor, partial_sol, left_side=True, lower=True, transpose_a=True
    )


def body(right_side, start_guess, couple_x, couple_y, couple_z, reaction):
    rows_x, rows_y, flat_len = right_side.shape
    layers = couple_z.shape[2]
    count_rhs = flat_len // layers
    plane = rows_y * layers
    depth = jnp.arange(plane, dtype=jnp.int32) % layers
    keep_first = (depth != 0).astype(jnp.float32)
    keep_last = (depth != layers - 1).astype(jnp.float32)

    def inward(values):
        split = values.reshape(rows_x, rows_y, count_rhs, layers)
        return jnp.transpose(split, (2, 0, 1, 3)).reshape(count_rhs, rows_x, plane)

    def outward(values):
        split = values.reshape(count_rhs, rows_x, rows_y, layers)
        return jnp.transpose(split, (1, 2, 0, 3)).reshape(rows_x, rows_y, flat_len)

    def coef(values):
        return values.reshape(1, rows_x, plane)

    def low_x(values):
        return low_along(values, 1, 1)

    def up_x(values):
        return up_along(values, 1, 1)

    def low_y(values):
        return low_along(values, 2, layers)

    def up_y(values):
        return up_along(values, 2, layers)

    def low_z(values):
        return low_along(values, 2, 1) * keep_first

    def up_z(values):
        return up_along(values, 2, 1) * keep_last

    def forward(block, axis):
        count = lax.axis_size(axis)
        return lax.ppermute(block, axis, [(i, i + 1) for i in range(count - 1)])

    def backward(block, axis):
        count = lax.axis_size(axis)
        return lax.ppermute(block, axis, [(i + 1, i) for i in range(count - 1)])

    after_x = coef(couple_x)
    after_y = coef(couple_y)
    after_z = coef(couple_z)
    edge_x = forward(after_x[:, -1:], "gx")
    edge_y = forward(after_y[:, :, plane - layers :], "gy")
    before_x = jnp.concatenate([edge_x, after_x[:, :-1]], axis=1)
    before_y = jnp.concatenate([edge_y, after_y[:, :, : plane - layers]], axis=2)
    before_z = low_z(after_z)
    diagonal = coef(reaction) + after_x + before_x + after_y + before_y + after_z + before_z

    def apply_op(values):
        from_low_x = forward(values[:, -1:], "gx")
        from_high_x = backward(values[:, :1], "gx")
        from_low_y = forward(values[:, :, plane - layers :], "gy")
        from_high_y = backward(values[:, :, :layers], "gy")
        next_x = jnp.concatenate([values[:, 1:], from_high_x], axis=1)
        prev_x = jnp.concatenate([from_low_x, values[:, :-1]], axis=1)
        next_y = jnp.concatenate([values[:, :, layers:], from_high_y], axis=2)
        prev_y = jnp.concatenate([from_low_y, values[:, :, : plane - layers]], axis=2)
        return (
            diagonal * values
            - after_x * next_x
            - before_x * prev_x
            - after_y * next_y
            - before_y * prev_y
            - after_z * up_z(values)
            - before_z * low_z(values)
        )

    lows = (low_x(after_x), low_y(after_y), before_z)
    ups = (
        up_x(jnp.ones_like(after_x)) * after_x,
        up_y(jnp.ones_like(after_y)) * after_y,
        after_z,
    )
    pivots = diagonal
    for repeat in range(FACT_SWEEPS):
        inv_now = 1.0 / pivots
        pivots = (
            diagonal
            - lows[0] * lows[0] * low_x(inv_now)
            - lows[1] * lows[1] * low_y(inv_now)
            - lows[2] * lows[2] * low_z(inv_now)
        )
    inv_piv = 1.0 / pivots

    def total_gram(former, latter):
        return mesh_sum(block_gram(former, latter))

    rhs_in = inward(right_side)
    start_in = inward(start_guess)
    start_res = rhs_in - apply_op(start_in)
    first_factor, first_inv = chol_factor(total_gram(start_res, start_res))
    basis_set = [mix_block(start_res, first_inv)]
    precond_set = []
    columns = []
    for column in range(ITERS):
        source = basis_set[column]
        lower_sol = inv_piv * source
        for precondition_repeat in range(SWEEPS):
            lower_sol = inv_piv * (
                source
                + lows[0] * low_x(lower_sol)
                + lows[1] * low_y(lower_sol)
                + lows[2] * low_z(lower_sol)
            )
        upper_sol = lower_sol
        for precondition_repeat in range(SWEEPS):
            upper_sol = lower_sol + inv_piv * (
                ups[0] * up_x(upper_sol)
                + ups[1] * up_y(upper_sol)
                + ups[2] * up_z(upper_sol)
            )
        image = apply_op(upper_sol)
        precond_set.append(upper_sol)
        local_proj = jnp.stack([block_gram(member, image) for member in basis_set])
        stacked = mesh_sum(local_proj)
        projections = [stacked[member] for member in range(len(basis_set))]
        removed = mix_block(basis_set[0], projections[0])
        for member in range(1, len(basis_set)):
            removed = removed + mix_block(basis_set[member], projections[member])
        perp = image - removed
        next_factor, next_inv = chol_factor(total_gram(perp, perp))
        if column + 1 < ITERS:
            basis_set.append(mix_block(perp, next_inv))
        blank = jnp.zeros(((ITERS - 1 - column) * count_rhs, count_rhs), dtype=next_factor.dtype)
        columns.append(jnp.concatenate(projections + [next_factor, blank], axis=0))
    coeffs = solve_small(columns, first_factor)
    solution = start_in
    for column in range(ITERS):
        solution = solution + mix_block(
            precond_set[column], coeffs[column * count_rhs : (column + 1) * count_rhs]
        )
    residual = rhs_in - apply_op(solution)
    return (outward(solution), outward(residual))


def solution(mesh):
    return jax.shard_map(
        body,
        mesh=mesh,
        in_specs=(
            P("gx", "gy", None),
            P("gx", "gy", None),
            P("gx", "gy", None),
            P("gx", "gy", None),
            P("gx", "gy", None),
            P("gx", "gy", None),
        ),
        out_specs=(P("gx", "gy", None), P("gx", "gy", None)),
        check_vma=False,
    )
```

```python
import jax
import jax.numpy as jnp
from jax import lax
from jax.sharding import PartitionSpec as P

ITERS = 2
SWEEPS = 4
FACT_SWEEPS = 3


HIGH = lax.Precision.HIGHEST


def mesh_sum(block):
    for axis in ("gx", "gy"):
        count = lax.axis_size(axis)
        if count & (count - 1):
            block = lax.psum(block, axis)
            continue
        step = 1
        while step < count:
            radix = 4 if count % (step * 4) == 0 else 2
            parts = [block] + [
                lax.ppermute(block, axis, [(i, i ^ (step * m)) for i in range(count)])
                for m in range(1, radix)
            ]
            while len(parts) > 1:
                parts = [parts[i] + parts[i + 1] for i in range(0, len(parts), 2)]
            block = parts[0]
            step *= radix
    return block


def low_along(values, axis, width):
    count = values.shape[axis]
    blank = jnp.zeros_like(lax.slice_in_dim(values, 0, width, axis=axis))
    return jnp.concatenate([blank, lax.slice_in_dim(values, 0, count - width, axis=axis)], axis=axis)


def up_along(values, axis, width):
    count = values.shape[axis]
    blank = jnp.zeros_like(lax.slice_in_dim(values, 0, width, axis=axis))
    return jnp.concatenate([lax.slice_in_dim(values, width, count, axis=axis), blank], axis=axis)


def block_gram(former, latter):
    return jnp.einsum("sxl,txl->st", former, latter, precision=HIGH)


def mix_block(values, matrix):
    return jnp.einsum("ts,sxl->txl", matrix.T, values, precision=HIGH)


def chol_factor(gram_mat):
    low_factor = jnp.linalg.cholesky(gram_mat)
    eye_mat = jnp.eye(gram_mat.shape[0], dtype=gram_mat.dtype)
    inverse = lax.linalg.triangular_solve(low_factor, eye_mat, left_side=True, lower=True)
    return (low_factor.T, inverse.T)


def solve_small(columns, first_factor):
    hessen = jnp.concatenate(columns, axis=1)
    count_rhs = first_factor.shape[0]
    target = jnp.dot(hessen[:count_rhs].T, first_factor, precision=HIGH)
    normal = jnp.dot(hessen.T, hessen, precision=HIGH)
    low_factor = jnp.linalg.cholesky(normal)
    partial_sol = lax.linalg.triangular_solve(low_factor, target, left_side=True, lower=True)
    return lax.linalg.triangular_solve(
        low_factor, partial_sol, left_side=True, lower=True, transpose_a=True
    )


def body(right_side, start_guess, couple_x, couple_y, couple_z, reaction):
    rows_x, rows_y, flat_len = right_side.shape
    layers = couple_z.shape[2]
    count_rhs = flat_len // layers
    plane = rows_y * layers
    depth = jnp.arange(plane, dtype=jnp.int32) % layers
    keep_first = (depth != 0).astype(jnp.float32)
    keep_last = (depth != layers - 1).astype(jnp.float32)

    def inward(values):
        split = values.reshape(rows_x, rows_y, count_rhs, layers)
        return jnp.transpose(split, (2, 0, 1, 3)).reshape(count_rhs, rows_x, plane)

    def outward(values):
        split = values.reshape(count_rhs, rows_x, rows_y, layers)
        return jnp.transpose(split, (1, 2, 0, 3)).reshape(rows_x, rows_y, flat_len)

    def coef(values):
        return values.reshape(1, rows_x, plane)

    def low_x(values):
        return low_along(values, 1, 1)

    def up_x(values):
        return up_along(values, 1, 1)

    def low_y(values):
        return low_along(values, 2, layers)

    def up_y(values):
        return up_along(values, 2, layers)

    def low_z(values):
        return low_along(values, 2, 1) * keep_first

    def up_z(values):
        return up_along(values, 2, 1) * keep_last

    def forward(block, axis):
        count = lax.axis_size(axis)
        return lax.ppermute(block, axis, [(i, i + 1) for i in range(count - 1)])

    def backward(block, axis):
        count = lax.axis_size(axis)
        return lax.ppermute(block, axis, [(i + 1, i) for i in range(count - 1)])

    after_x = coef(couple_x)
    after_y = coef(couple_y)
    after_z = coef(couple_z)
    edge_x = forward(after_x[:, -1:], "gx")
    edge_y = forward(after_y[:, :, plane - layers :], "gy")
    before_x = jnp.concatenate([edge_x, after_x[:, :-1]], axis=1)
    before_y = jnp.concatenate([edge_y, after_y[:, :, : plane - layers]], axis=2)
    before_z = low_z(after_z)
    diagonal = coef(reaction) + after_x + before_x + after_y + before_y + after_z + before_z

    def halos(values):
        return (
            forward(values[:, -1:], "gx"),
            backward(values[:, :1], "gx"),
            forward(values[:, :, plane - layers :], "gy"),
            backward(values[:, :, :layers], "gy"),
        )

    def apply_op(values, edges):
        from_low_x, from_high_x, from_low_y, from_high_y = edges
        next_x = jnp.concatenate([values[:, 1:], from_high_x], axis=1)
        prev_x = jnp.concatenate([from_low_x, values[:, :-1]], axis=1)
        next_y = jnp.concatenate([values[:, :, layers:], from_high_y], axis=2)
        prev_y = jnp.concatenate([from_low_y, values[:, :, : plane - layers]], axis=2)
        return (
            diagonal * values
            - after_x * next_x
            - before_x * prev_x
            - after_y * next_y
            - before_y * prev_y
            - after_z * up_z(values)
            - before_z * low_z(values)
        )

    lows = (low_x(after_x), low_y(after_y), before_z)
    ups = (
        up_x(jnp.ones_like(after_x)) * after_x,
        up_y(jnp.ones_like(after_y)) * after_y,
        after_z,
    )
    pivots = diagonal
    for repeat in range(FACT_SWEEPS):
        inv_now = 1.0 / pivots
        pivots = (
            diagonal
            - lows[0] * lows[0] * low_x(inv_now)
            - lows[1] * lows[1] * low_y(inv_now)
            - lows[2] * lows[2] * low_z(inv_now)
        )
    inv_piv = 1.0 / pivots

    def total_gram(former, latter):
        return mesh_sum(block_gram(former, latter))

    rhs_in = inward(right_side)
    start_in = inward(start_guess)
    start_edges = halos(start_in)
    start_res = rhs_in - apply_op(start_in, start_edges)
    first_factor, first_inv = chol_factor(total_gram(start_res, start_res))
    basis_set = [mix_block(start_res, first_inv)]
    basis_grams = {}
    precond_set = []
    edge_set = []
    columns = []
    for column in range(ITERS):
        source = basis_set[column]
        lower_sol = inv_piv * source
        for precondition_repeat in range(SWEEPS):
            lower_sol = inv_piv * (
                source
                + lows[0] * low_x(lower_sol)
                + lows[1] * low_y(lower_sol)
                + lows[2] * low_z(lower_sol)
            )
        upper_sol = lower_sol
        for precondition_repeat in range(SWEEPS):
            upper_sol = lower_sol + inv_piv * (
                ups[0] * up_x(upper_sol)
                + ups[1] * up_y(upper_sol)
                + ups[2] * up_z(upper_sol)
            )
        upper_edges = halos(upper_sol)
        image = apply_op(upper_sol, upper_edges)
        precond_set.append(upper_sol)
        edge_set.append(upper_edges)
        count = len(basis_set)
        new_pairs = [(i, k) for k in range(count) for i in range(k + 1) if (i, k) not in basis_grams]
        local = [block_gram(member, image) for member in basis_set]
        local.append(block_gram(image, image))
        local += [block_gram(basis_set[i], basis_set[k]) for i, k in new_pairs]
        stacked = mesh_sum(jnp.stack(local))
        projections = [stacked[member] for member in range(count)]
        image_gram = stacked[count]
        for slot, pair in enumerate(new_pairs):
            basis_grams[pair] = stacked[count + 1 + slot]
        removed = mix_block(basis_set[0], projections[0])
        for member in range(1, count):
            removed = removed + mix_block(basis_set[member], projections[member])
        perp = image - removed
        cross = sum(jnp.dot(h.T, h, precision=HIGH) for h in projections)
        spread = 0.0
        for i in range(count):
            for k in range(count):
                pair_gram = basis_grams[(i, k)] if i <= k else basis_grams[(k, i)].T
                spread = spread + jnp.dot(
                    projections[i].T, jnp.dot(pair_gram, projections[k], precision=HIGH), precision=HIGH
                )
        perp_gram = image_gram - cross - cross + spread
        next_factor, next_inv = chol_factor(perp_gram)
        if column + 1 < ITERS:
            basis_set.append(mix_block(perp, next_inv))
        blank = jnp.zeros(((ITERS - 1 - column) * count_rhs, count_rhs), dtype=next_factor.dtype)
        columns.append(jnp.concatenate(projections + [next_factor, blank], axis=0))
    coeffs = solve_small(columns, first_factor)
    solution = start_in
    solution_edges = start_edges
    for column in range(ITERS):
        weights = coeffs[column * count_rhs : (column + 1) * count_rhs]
        solution = solution + mix_block(precond_set[column], weights)
        solution_edges = tuple(
            have + mix_block(extra, weights)
            for have, extra in zip(solution_edges, edge_set[column])
        )
    residual = rhs_in - apply_op(solution, solution_edges)
    return (outward(solution), outward(residual))


def solution(mesh):
    return jax.shard_map(
        body,
        mesh=mesh,
        in_specs=(
            P("gx", "gy", None),
            P("gx", "gy", None),
            P("gx", "gy", None),
            P("gx", "gy", None),
            P("gx", "gy", None),
            P("gx", "gy", None),
        ),
        out_specs=(P("gx", "gy", None), P("gx", "gy", None)),
        check_vma=False,
    )
```

```python
import jax
import jax.numpy as jnp
from jax import lax
from jax.sharding import PartitionSpec as P

ITERS = 2
SWEEPS = 4
FACT_SWEEPS = 3
SHIFT = 1.0


HIGH = lax.Precision.HIGHEST


def mesh_sum(block):
    for axis in ("gx", "gy"):
        count = lax.axis_size(axis)
        if count & (count - 1):
            block = lax.psum(block, axis)
            continue
        step = 1
        while step < count:
            radix = 4 if count % (step * 4) == 0 else 2
            parts = [block] + [
                lax.ppermute(block, axis, [(i, i ^ (step * m)) for i in range(count)])
                for m in range(1, radix)
            ]
            while len(parts) > 1:
                parts = [parts[i] + parts[i + 1] for i in range(0, len(parts), 2)]
            block = parts[0]
            step *= radix
    return block


def low_along(values, axis, width):
    count = values.shape[axis]
    blank = jnp.zeros_like(lax.slice_in_dim(values, 0, width, axis=axis))
    return jnp.concatenate([blank, lax.slice_in_dim(values, 0, count - width, axis=axis)], axis=axis)


def up_along(values, axis, width):
    count = values.shape[axis]
    blank = jnp.zeros_like(lax.slice_in_dim(values, 0, width, axis=axis))
    return jnp.concatenate([lax.slice_in_dim(values, width, count, axis=axis), blank], axis=axis)


def block_gram(former, latter):
    return jnp.einsum("sxl,txl->st", former, latter, precision=HIGH)


def mix_block(values, matrix):
    return jnp.einsum("ts,sxl->txl", matrix.T, values, precision=HIGH)


def chol_factor(gram_mat):
    low_factor = jnp.linalg.cholesky(gram_mat)
    eye_mat = jnp.eye(gram_mat.shape[0], dtype=gram_mat.dtype)
    inverse = lax.linalg.triangular_solve(low_factor, eye_mat, left_side=True, lower=True)
    return (low_factor.T, inverse.T)


def solve_small(columns, first_factor):
    hessen = jnp.concatenate(columns, axis=1)
    count_rhs = first_factor.shape[0]
    target = jnp.dot(hessen[:count_rhs].T, first_factor, precision=HIGH)
    normal = jnp.dot(hessen.T, hessen, precision=HIGH)
    low_factor = jnp.linalg.cholesky(normal)
    partial_sol = lax.linalg.triangular_solve(low_factor, target, left_side=True, lower=True)
    return lax.linalg.triangular_solve(
        low_factor, partial_sol, left_side=True, lower=True, transpose_a=True
    )


def body(right_side, start_guess, couple_x, couple_y, couple_z, reaction):
    rows_x, rows_y, flat_len = right_side.shape
    layers = couple_z.shape[2]
    count_rhs = flat_len // layers
    plane = rows_y * layers
    depth = jnp.arange(plane, dtype=jnp.int32) % layers
    keep_first = (depth != 0).astype(jnp.float32)
    keep_last = (depth != layers - 1).astype(jnp.float32)

    def inward(values):
        split = values.reshape(rows_x, rows_y, count_rhs, layers)
        return jnp.transpose(split, (2, 0, 1, 3)).reshape(count_rhs, rows_x, plane)

    def outward(values):
        split = values.reshape(count_rhs, rows_x, rows_y, layers)
        return jnp.transpose(split, (1, 2, 0, 3)).reshape(rows_x, rows_y, flat_len)

    def coef(values):
        return values.reshape(1, rows_x, plane)

    def low_x(values):
        return low_along(values, 1, 1)

    def up_x(values):
        return up_along(values, 1, 1)

    def low_y(values):
        return low_along(values, 2, layers)

    def up_y(values):
        return up_along(values, 2, layers)

    def low_z(values):
        return low_along(values, 2, 1) * keep_first

    def up_z(values):
        return up_along(values, 2, 1) * keep_last

    def forward(block, axis):
        count = lax.axis_size(axis)
        return lax.ppermute(block, axis, [(i, i + 1) for i in range(count - 1)])

    def backward(block, axis):
        count = lax.axis_size(axis)
        return lax.ppermute(block, axis, [(i + 1, i) for i in range(count - 1)])

    after_x = coef(couple_x)
    after_y = coef(couple_y)
    after_z = coef(couple_z)
    edge_x = forward(after_x[:, -1:], "gx")
    edge_y = forward(after_y[:, :, plane - layers :], "gy")
    before_x = jnp.concatenate([edge_x, after_x[:, :-1]], axis=1)
    before_y = jnp.concatenate([edge_y, after_y[:, :, : plane - layers]], axis=2)
    before_z = low_z(after_z)
    diagonal = coef(reaction) + after_x + before_x + after_y + before_y + after_z + before_z

    def halos(values):
        return (
            forward(values[:, -1:], "gx"),
            backward(values[:, :1], "gx"),
            forward(values[:, :, plane - layers :], "gy"),
            backward(values[:, :, :layers], "gy"),
        )

    def apply_op(values, edges):
        from_low_x, from_high_x, from_low_y, from_high_y = edges
        next_x = jnp.concatenate([values[:, 1:], from_high_x], axis=1)
        prev_x = jnp.concatenate([from_low_x, values[:, :-1]], axis=1)
        next_y = jnp.concatenate([values[:, :, layers:], from_high_y], axis=2)
        prev_y = jnp.concatenate([from_low_y, values[:, :, : plane - layers]], axis=2)
        return (
            diagonal * values
            - after_x * next_x
            - before_x * prev_x
            - after_y * next_y
            - before_y * prev_y
            - after_z * up_z(values)
            - before_z * low_z(values)
        )

    lows = (low_x(after_x), low_y(after_y), before_z)
    ups = (
        up_x(jnp.ones_like(after_x)) * after_x,
        up_y(jnp.ones_like(after_y)) * after_y,
        after_z,
    )
    pivots = diagonal
    for repeat in range(FACT_SWEEPS):
        inv_now = 1.0 / pivots
        pivots = (
            diagonal
            - lows[0] * lows[0] * low_x(inv_now)
            - lows[1] * lows[1] * low_y(inv_now)
            - lows[2] * lows[2] * low_z(inv_now)
        )
    inv_piv = 1.0 / pivots

    def total_gram(former, latter):
        return mesh_sum(block_gram(former, latter))

    rhs_in = inward(right_side)
    start_in = inward(start_guess)
    def precondition(source):
        lower_sol = inv_piv * source
        for precondition_repeat in range(SWEEPS):
            lower_sol = inv_piv * (
                source
                + lows[0] * low_x(lower_sol)
                + lows[1] * low_y(lower_sol)
                + lows[2] * low_z(lower_sol)
            )
        upper_sol = lower_sol
        for precondition_repeat in range(SWEEPS):
            upper_sol = lower_sol + inv_piv * (
                ups[0] * up_x(upper_sol)
                + ups[1] * up_y(upper_sol)
                + ups[2] * up_z(upper_sol)
            )
        return upper_sol

    start_edges = halos(start_in)
    start_res = rhs_in - apply_op(start_in, start_edges)
    krylov = [start_res]
    precond_set = []
    edge_set = []
    for column in range(ITERS):
        turned = precondition(krylov[-1])
        turned_edges = halos(turned)
        precond_set.append(turned)
        edge_set.append(turned_edges)
        krylov.append(apply_op(turned, turned_edges) - SHIFT * krylov[-1])
    stacked = jnp.concatenate(krylov, axis=0)
    span_gram = mesh_sum(block_gram(stacked, stacked))
    width = span_gram.shape[0]

    def inner(left, right):
        return jnp.dot(left.T, jnp.dot(span_gram, right, precision=HIGH), precision=HIGH)

    def advance(weights):
        moved = jnp.concatenate([jnp.zeros_like(weights[:count_rhs]), weights[:-count_rhs]], axis=0)
        return moved + SHIFT * weights

    first_factor, first_inv = chol_factor(inner(*(2 * [jnp.eye(width, count_rhs, dtype=jnp.float32)])))
    basis_set = [jnp.dot(jnp.eye(width, count_rhs, dtype=jnp.float32), first_inv, precision=HIGH)]
    columns = []
    for column in range(ITERS):
        image = advance(basis_set[column])
        projections = [inner(member, image) for member in basis_set]
        perp = image - sum(
            jnp.dot(member, proj, precision=HIGH) for member, proj in zip(basis_set, projections)
        )
        next_factor, next_inv = chol_factor(inner(perp, perp))
        if column + 1 < ITERS:
            basis_set.append(jnp.dot(perp, next_inv, precision=HIGH))
        blank = jnp.zeros(((ITERS - 1 - column) * count_rhs, count_rhs), dtype=next_factor.dtype)
        columns.append(jnp.concatenate(projections + [next_factor, blank], axis=0))
    coeffs = solve_small(columns, first_factor)
    combined = sum(
        jnp.dot(basis_set[column], coeffs[column * count_rhs : (column + 1) * count_rhs], precision=HIGH)
        for column in range(ITERS)
    )
    solution = start_in
    solution_edges = start_edges
    for column in range(ITERS):
        weights = combined[column * count_rhs : (column + 1) * count_rhs]
        solution = solution + mix_block(precond_set[column], weights)
        solution_edges = tuple(
            have + mix_block(extra, weights)
            for have, extra in zip(solution_edges, edge_set[column])
        )
    residual = rhs_in - apply_op(solution, solution_edges)
    return (outward(solution), outward(residual))


def solution(mesh):
    return jax.shard_map(
        body,
        mesh=mesh,
        in_specs=(
            P("gx", "gy", None),
            P("gx", "gy", None),
            P("gx", "gy", None),
            P("gx", "gy", None),
            P("gx", "gy", None),
            P("gx", "gy", None),
        ),
        out_specs=(P("gx", "gy", None), P("gx", "gy", None)),
        check_vma=False,
    )
```

```python
import jax
import jax.numpy as jnp
from jax import lax
from jax.sharding import PartitionSpec as P

ITERS = 2
SWEEPS = 4
FACT_SWEEPS = 3
SHIFT = 1.0


HIGH = lax.Precision.HIGHEST


def mesh_sum(block):
    for axis in ("gx", "gy"):
        count = lax.axis_size(axis)
        if count & (count - 1):
            block = lax.psum(block, axis)
            continue
        step = 1
        while step < count:
            radix = 4 if count % (step * 4) == 0 else 2
            parts = [block] + [
                lax.ppermute(block, axis, [(i, i ^ (step * m)) for i in range(count)])
                for m in range(1, radix)
            ]
            while len(parts) > 1:
                parts = [parts[i] + parts[i + 1] for i in range(0, len(parts), 2)]
            block = parts[0]
            step *= radix
    return block


def low_along(values, axis, width):
    count = values.shape[axis]
    blank = jnp.zeros_like(lax.slice_in_dim(values, 0, width, axis=axis))
    return jnp.concatenate([blank, lax.slice_in_dim(values, 0, count - width, axis=axis)], axis=axis)


def up_along(values, axis, width):
    count = values.shape[axis]
    blank = jnp.zeros_like(lax.slice_in_dim(values, 0, width, axis=axis))
    return jnp.concatenate([lax.slice_in_dim(values, width, count, axis=axis), blank], axis=axis)


def block_gram(former, latter):
    return jnp.einsum("sxl,txl->st", former, latter, precision=HIGH)


def mix_block(values, matrix):
    return jnp.einsum("ts,sxl->txl", matrix.T, values, precision=HIGH)


def chol_factor(gram_mat):
    low_factor = jnp.linalg.cholesky(gram_mat)
    eye_mat = jnp.eye(gram_mat.shape[0], dtype=gram_mat.dtype)
    inverse = lax.linalg.triangular_solve(low_factor, eye_mat, left_side=True, lower=True)
    return (low_factor.T, inverse.T)


def solve_small(columns, first_factor):
    hessen = jnp.concatenate(columns, axis=1)
    count_rhs = first_factor.shape[0]
    target = jnp.dot(hessen[:count_rhs].T, first_factor, precision=HIGH)
    normal = jnp.dot(hessen.T, hessen, precision=HIGH)
    low_factor = jnp.linalg.cholesky(normal)
    partial_sol = lax.linalg.triangular_solve(low_factor, target, left_side=True, lower=True)
    return lax.linalg.triangular_solve(
        low_factor, partial_sol, left_side=True, lower=True, transpose_a=True
    )


def body(right_side, start_guess, couple_x, couple_y, couple_z, reaction):
    rows_x, rows_y, flat_len = right_side.shape
    layers = couple_z.shape[2]
    count_rhs = flat_len // layers
    plane = rows_y * layers
    depth = jnp.arange(plane, dtype=jnp.int32) % layers
    keep_first = (depth != 0).astype(jnp.float32)
    keep_last = (depth != layers - 1).astype(jnp.float32)

    def inward(values):
        split = values.reshape(rows_x, rows_y, count_rhs, layers)
        return jnp.transpose(split, (2, 0, 1, 3)).reshape(count_rhs, rows_x, plane)

    def outward(values):
        split = values.reshape(count_rhs, rows_x, rows_y, layers)
        return jnp.transpose(split, (1, 2, 0, 3)).reshape(rows_x, rows_y, flat_len)

    def coef(values):
        return values.reshape(1, rows_x, plane)

    def low_x(values):
        return low_along(values, 1, 1)

    def up_x(values):
        return up_along(values, 1, 1)

    def low_y(values):
        return low_along(values, 2, layers)

    def up_y(values):
        return up_along(values, 2, layers)

    def low_z(values):
        return low_along(values, 2, 1) * keep_first

    def up_z(values):
        return up_along(values, 2, 1) * keep_last

    def forward(block, axis):
        count = lax.axis_size(axis)
        return lax.ppermute(block, axis, [(i, i + 1) for i in range(count - 1)])

    def backward(block, axis):
        count = lax.axis_size(axis)
        return lax.ppermute(block, axis, [(i + 1, i) for i in range(count - 1)])

    after_x = coef(couple_x)
    after_y = coef(couple_y)
    after_z = coef(couple_z)
    edge_x = forward(after_x[:, -1:], "gx")
    edge_y = forward(after_y[:, :, plane - layers :], "gy")
    before_x = jnp.concatenate([edge_x, after_x[:, :-1]], axis=1)
    before_y = jnp.concatenate([edge_y, after_y[:, :, : plane - layers]], axis=2)
    before_z = low_z(after_z)
    diagonal = coef(reaction) + after_x + before_x + after_y + before_y + after_z + before_z

    def packed(slab):
        return slab.reshape(count_rhs, rows_x * layers // 128, 128)

    def unpacked(slab):
        return slab.reshape(count_rhs, rows_x, layers)

    def halos(values):
        return (
            forward(values[:, -1:], "gx"),
            backward(values[:, :1], "gx"),
            unpacked(forward(packed(values[:, :, plane - layers :]), "gy")),
            unpacked(backward(packed(values[:, :, :layers]), "gy")),
        )

    def apply_op(values, edges):
        from_low_x, from_high_x, from_low_y, from_high_y = edges
        next_x = jnp.concatenate([values[:, 1:], from_high_x], axis=1)
        prev_x = jnp.concatenate([from_low_x, values[:, :-1]], axis=1)
        next_y = jnp.concatenate([values[:, :, layers:], from_high_y], axis=2)
        prev_y = jnp.concatenate([from_low_y, values[:, :, : plane - layers]], axis=2)
        return (
            diagonal * values
            - after_x * next_x
            - before_x * prev_x
            - after_y * next_y
            - before_y * prev_y
            - after_z * up_z(values)
            - before_z * low_z(values)
        )

    lows = (low_x(after_x), low_y(after_y), before_z)
    ups = (
        up_x(jnp.ones_like(after_x)) * after_x,
        up_y(jnp.ones_like(after_y)) * after_y,
        after_z,
    )
    pivots = diagonal
    for repeat in range(FACT_SWEEPS):
        inv_now = 1.0 / pivots
        pivots = (
            diagonal
            - lows[0] * lows[0] * low_x(inv_now)
            - lows[1] * lows[1] * low_y(inv_now)
            - lows[2] * lows[2] * low_z(inv_now)
        )
    inv_piv = 1.0 / pivots

    def total_gram(former, latter):
        return mesh_sum(block_gram(former, latter))

    rhs_in = inward(right_side)
    start_in = inward(start_guess)
    def precondition(source):
        lower_sol = inv_piv * source
        for precondition_repeat in range(SWEEPS):
            lower_sol = inv_piv * (
                source
                + lows[0] * low_x(lower_sol)
                + lows[1] * low_y(lower_sol)
                + lows[2] * low_z(lower_sol)
            )
        upper_sol = lower_sol
        for precondition_repeat in range(SWEEPS):
            upper_sol = lower_sol + inv_piv * (
                ups[0] * up_x(upper_sol)
                + ups[1] * up_y(upper_sol)
                + ups[2] * up_z(upper_sol)
            )
        return upper_sol

    start_edges = halos(start_in)
    start_res = rhs_in - apply_op(start_in, start_edges)
    krylov = [start_res]
    precond_set = []
    edge_set = []
    for column in range(ITERS):
        turned = precondition(krylov[-1])
        turned_edges = halos(turned)
        precond_set.append(turned)
        edge_set.append(turned_edges)
        krylov.append(apply_op(turned, turned_edges) - SHIFT * krylov[-1])
    stacked = jnp.concatenate(krylov, axis=0)
    local_gram = block_gram(stacked, stacked)
    count_blocks = len(krylov)
    pairs = [(i, k) for i in range(count_blocks) for k in range(i, count_blocks)]
    upper = mesh_sum(
        jnp.stack(
            [
                local_gram[i * count_rhs : (i + 1) * count_rhs, k * count_rhs : (k + 1) * count_rhs]
                for i, k in pairs
            ]
        )
    )
    span_gram = jnp.concatenate(
        [
            jnp.concatenate(
                [upper[pairs.index((i, k))] if i <= k else upper[pairs.index((k, i))].T for k in range(count_blocks)],
                axis=1,
            )
            for i in range(count_blocks)
        ],
        axis=0,
    )
    width = span_gram.shape[0]

    def inner(left, right):
        return jnp.dot(left.T, jnp.dot(span_gram, right, precision=HIGH), precision=HIGH)

    def advance(weights):
        moved = jnp.concatenate([jnp.zeros_like(weights[:count_rhs]), weights[:-count_rhs]], axis=0)
        return moved + SHIFT * weights

    first_factor, first_inv = chol_factor(inner(*(2 * [jnp.eye(width, count_rhs, dtype=jnp.float32)])))
    basis_set = [jnp.dot(jnp.eye(width, count_rhs, dtype=jnp.float32), first_inv, precision=HIGH)]
    columns = []
    for column in range(ITERS):
        image = advance(basis_set[column])
        projections = [inner(member, image) for member in basis_set]
        perp = image - sum(
            jnp.dot(member, proj, precision=HIGH) for member, proj in zip(basis_set, projections)
        )
        next_factor, next_inv = chol_factor(inner(perp, perp))
        if column + 1 < ITERS:
            basis_set.append(jnp.dot(perp, next_inv, precision=HIGH))
        blank = jnp.zeros(((ITERS - 1 - column) * count_rhs, count_rhs), dtype=next_factor.dtype)
        columns.append(jnp.concatenate(projections + [next_factor, blank], axis=0))
    coeffs = solve_small(columns, first_factor)
    combined = sum(
        jnp.dot(basis_set[column], coeffs[column * count_rhs : (column + 1) * count_rhs], precision=HIGH)
        for column in range(ITERS)
    )
    solution = start_in
    solution_edges = start_edges
    for column in range(ITERS):
        weights = combined[column * count_rhs : (column + 1) * count_rhs]
        solution = solution + mix_block(precond_set[column], weights)
        solution_edges = tuple(
            have + mix_block(extra, weights)
            for have, extra in zip(solution_edges, edge_set[column])
        )
    residual = rhs_in - apply_op(solution, solution_edges)
    return (outward(solution), outward(residual))


def solution(mesh):
    return jax.shard_map(
        body,
        mesh=mesh,
        in_specs=(
            P("gx", "gy", None),
            P("gx", "gy", None),
            P("gx", "gy", None),
            P("gx", "gy", None),
            P("gx", "gy", None),
            P("gx", "gy", None),
        ),
        out_specs=(P("gx", "gy", None), P("gx", "gy", None)),
        check_vma=False,
    )
```

```python
import jax
import jax.numpy as jnp
from jax import lax
from jax.sharding import PartitionSpec as P

ITERS = 2
SWEEPS = 4
FACT_SWEEPS = 3
SHIFT = 1.0


HIGH = lax.Precision.HIGHEST


def mesh_sum(block):
    for axis in ("gx", "gy"):
        count = lax.axis_size(axis)
        if count & (count - 1):
            block = lax.psum(block, axis)
            continue
        step = 1
        while step < count:
            radix = 4 if count % (step * 4) == 0 else 2
            parts = [block] + [
                lax.ppermute(block, axis, [(i, i ^ (step * m)) for i in range(count)])
                for m in range(1, radix)
            ]
            while len(parts) > 1:
                parts = [parts[i] + parts[i + 1] for i in range(0, len(parts), 2)]
            block = parts[0]
            step *= radix
    return block


def low_along(values, axis, width):
    count = values.shape[axis]
    blank = jnp.zeros_like(lax.slice_in_dim(values, 0, width, axis=axis))
    return jnp.concatenate([blank, lax.slice_in_dim(values, 0, count - width, axis=axis)], axis=axis)


def up_along(values, axis, width):
    count = values.shape[axis]
    blank = jnp.zeros_like(lax.slice_in_dim(values, 0, width, axis=axis))
    return jnp.concatenate([lax.slice_in_dim(values, width, count, axis=axis), blank], axis=axis)


def block_gram(former, latter):
    return jnp.einsum("sxl,txl->st", former, latter, precision=HIGH)


def mix_block(values, matrix):
    return jnp.einsum("ts,sxl->txl", matrix.T, values, precision=HIGH)


def chol_factor(gram_mat):
    low_factor = jnp.linalg.cholesky(gram_mat)
    eye_mat = jnp.eye(gram_mat.shape[0], dtype=gram_mat.dtype)
    inverse = lax.linalg.triangular_solve(low_factor, eye_mat, left_side=True, lower=True)
    return (low_factor.T, inverse.T)


def solve_small(columns, first_factor):
    hessen = jnp.concatenate(columns, axis=1)
    count_rhs = first_factor.shape[0]
    target = jnp.dot(hessen[:count_rhs].T, first_factor, precision=HIGH)
    normal = jnp.dot(hessen.T, hessen, precision=HIGH)
    low_factor = jnp.linalg.cholesky(normal)
    partial_sol = lax.linalg.triangular_solve(low_factor, target, left_side=True, lower=True)
    return lax.linalg.triangular_solve(
        low_factor, partial_sol, left_side=True, lower=True, transpose_a=True
    )


def body(right_side, start_guess, couple_x, couple_y, couple_z, reaction):
    rows_x, rows_y, flat_len = right_side.shape
    layers = couple_z.shape[2]
    count_rhs = flat_len // layers
    plane = rows_y * layers
    depth = jnp.arange(plane, dtype=jnp.int32) % layers
    keep_first = (depth != 0).astype(jnp.float32)
    keep_last = (depth != layers - 1).astype(jnp.float32)

    def inward(values):
        split = values.reshape(rows_x, rows_y, count_rhs, layers)
        return jnp.transpose(split, (2, 0, 1, 3)).reshape(count_rhs, rows_x, plane)

    def outward(values):
        split = values.reshape(count_rhs, rows_x, rows_y, layers)
        return jnp.transpose(split, (1, 2, 0, 3)).reshape(rows_x, rows_y, flat_len)

    def coef(values):
        return values.reshape(1, rows_x, plane)

    def low_x(values):
        return low_along(values, 1, 1)

    def up_x(values):
        return up_along(values, 1, 1)

    def low_y(values):
        return low_along(values, 2, layers)

    def up_y(values):
        return up_along(values, 2, layers)

    def low_z(values):
        return low_along(values, 2, 1) * keep_first

    def up_z(values):
        return up_along(values, 2, 1) * keep_last

    def forward(block, axis):
        count = lax.axis_size(axis)
        return lax.ppermute(block, axis, [(i, i + 1) for i in range(count - 1)])

    def backward(block, axis):
        count = lax.axis_size(axis)
        return lax.ppermute(block, axis, [(i + 1, i) for i in range(count - 1)])

    after_x = coef(couple_x)
    after_y = coef(couple_y)
    after_z = coef(couple_z)
    edge_x = forward(after_x[:, -1:], "gx")
    edge_y = forward(after_y[:, :, plane - layers :], "gy")
    before_x = jnp.concatenate([edge_x, after_x[:, :-1]], axis=1)
    before_y = jnp.concatenate([edge_y, after_y[:, :, : plane - layers]], axis=2)
    before_z = low_z(after_z)
    diagonal = coef(reaction) + after_x + before_x + after_y + before_y + after_z + before_z

    def split_send(move, slab, axis):
        pieces = max(1, slab.size * 4 // 32768)
        if count_rhs % pieces:
            return move(slab, axis)
        share = count_rhs // pieces
        return jnp.concatenate(
            [move(slab[i * share : (i + 1) * share], axis) for i in range(pieces)], axis=0
        )

    def halos(values):
        return (
            split_send(forward, values[:, -1:], "gx"),
            split_send(backward, values[:, :1], "gx"),
            split_send(forward, values[:, :, plane - layers :], "gy"),
            split_send(backward, values[:, :, :layers], "gy"),
        )

    def apply_op(values, edges):
        from_low_x, from_high_x, from_low_y, from_high_y = edges
        next_x = jnp.concatenate([values[:, 1:], from_high_x], axis=1)
        prev_x = jnp.concatenate([from_low_x, values[:, :-1]], axis=1)
        next_y = jnp.concatenate([values[:, :, layers:], from_high_y], axis=2)
        prev_y = jnp.concatenate([from_low_y, values[:, :, : plane - layers]], axis=2)
        return (
            diagonal * values
            - after_x * next_x
            - before_x * prev_x
            - after_y * next_y
            - before_y * prev_y
            - after_z * up_z(values)
            - before_z * low_z(values)
        )

    lows = (low_x(after_x), low_y(after_y), before_z)
    ups = (
        up_x(jnp.ones_like(after_x)) * after_x,
        up_y(jnp.ones_like(after_y)) * after_y,
        after_z,
    )
    pivots = diagonal
    for repeat in range(FACT_SWEEPS):
        inv_now = 1.0 / pivots
        pivots = (
            diagonal
            - lows[0] * lows[0] * low_x(inv_now)
            - lows[1] * lows[1] * low_y(inv_now)
            - lows[2] * lows[2] * low_z(inv_now)
        )
    inv_piv = 1.0 / pivots

    def total_gram(former, latter):
        return mesh_sum(block_gram(former, latter))

    rhs_in = inward(right_side)
    start_in = inward(start_guess)
    def precondition(source):
        lower_sol = inv_piv * source
        for precondition_repeat in range(SWEEPS):
            lower_sol = inv_piv * (
                source
                + lows[0] * low_x(lower_sol)
                + lows[1] * low_y(lower_sol)
                + lows[2] * low_z(lower_sol)
            )
        upper_sol = lower_sol
        for precondition_repeat in range(SWEEPS):
            upper_sol = lower_sol + inv_piv * (
                ups[0] * up_x(upper_sol)
                + ups[1] * up_y(upper_sol)
                + ups[2] * up_z(upper_sol)
            )
        return upper_sol

    start_edges = halos(start_in)
    start_res = rhs_in - apply_op(start_in, start_edges)
    krylov = [start_res]
    precond_set = []
    edge_set = []
    for column in range(ITERS):
        turned = precondition(krylov[-1])
        turned_edges = halos(turned)
        precond_set.append(turned)
        edge_set.append(turned_edges)
        krylov.append(apply_op(turned, turned_edges) - SHIFT * krylov[-1])
    stacked = jnp.concatenate(krylov, axis=0)
    span_gram = mesh_sum(block_gram(stacked, stacked))
    width = span_gram.shape[0]

    def inner(left, right):
        return jnp.dot(left.T, jnp.dot(span_gram, right, precision=HIGH), precision=HIGH)

    def advance(weights):
        moved = jnp.concatenate([jnp.zeros_like(weights[:count_rhs]), weights[:-count_rhs]], axis=0)
        return moved + SHIFT * weights

    first_factor, first_inv = chol_factor(inner(*(2 * [jnp.eye(width, count_rhs, dtype=jnp.float32)])))
    basis_set = [jnp.dot(jnp.eye(width, count_rhs, dtype=jnp.float32), first_inv, precision=HIGH)]
    columns = []
    for column in range(ITERS):
        image = advance(basis_set[column])
        projections = [inner(member, image) for member in basis_set]
        perp = image - sum(
            jnp.dot(member, proj, precision=HIGH) for member, proj in zip(basis_set, projections)
        )
        next_factor, next_inv = chol_factor(inner(perp, perp))
        if column + 1 < ITERS:
            basis_set.append(jnp.dot(perp, next_inv, precision=HIGH))
        blank = jnp.zeros(((ITERS - 1 - column) * count_rhs, count_rhs), dtype=next_factor.dtype)
        columns.append(jnp.concatenate(projections + [next_factor, blank], axis=0))
    coeffs = solve_small(columns, first_factor)
    combined = sum(
        jnp.dot(basis_set[column], coeffs[column * count_rhs : (column + 1) * count_rhs], precision=HIGH)
        for column in range(ITERS)
    )
    solution = start_in
    solution_edges = start_edges
    for column in range(ITERS):
        weights = combined[column * count_rhs : (column + 1) * count_rhs]
        solution = solution + mix_block(precond_set[column], weights)
        solution_edges = tuple(
            have + mix_block(extra, weights)
            for have, extra in zip(solution_edges, edge_set[column])
        )
    residual = rhs_in - apply_op(solution, solution_edges)
    return (outward(solution), outward(residual))


def solution(mesh):
    return jax.shard_map(
        body,
        mesh=mesh,
        in_specs=(
            P("gx", "gy", None),
            P("gx", "gy", None),
            P("gx", "gy", None),
            P("gx", "gy", None),
            P("gx", "gy", None),
            P("gx", "gy", None),
        ),
        out_specs=(P("gx", "gy", None), P("gx", "gy", None)),
        check_vma=False,
    )
```

```python
import jax
import jax.numpy as jnp
from jax import lax
from jax.sharding import PartitionSpec as P

ITERS = 2
SWEEPS = 4
FACT_SWEEPS = 3
SHIFT = 1.0


HIGH = lax.Precision.HIGHEST


def mesh_sum(block):
    for axis in ("gx", "gy"):
        count = lax.axis_size(axis)
        if count & (count - 1):
            block = lax.psum(block, axis)
            continue
        step = 1
        while step < count:
            radix = 4 if count % (step * 4) == 0 else 2
            parts = [block] + [
                lax.ppermute(block, axis, [(i, i ^ (step * m)) for i in range(count)])
                for m in range(1, radix)
            ]
            while len(parts) > 1:
                parts = [parts[i] + parts[i + 1] for i in range(0, len(parts), 2)]
            block = parts[0]
            step *= radix
    return block


def low_along(values, axis, width):
    count = values.shape[axis]
    blank = jnp.zeros_like(lax.slice_in_dim(values, 0, width, axis=axis))
    return jnp.concatenate([blank, lax.slice_in_dim(values, 0, count - width, axis=axis)], axis=axis)


def up_along(values, axis, width):
    count = values.shape[axis]
    blank = jnp.zeros_like(lax.slice_in_dim(values, 0, width, axis=axis))
    return jnp.concatenate([lax.slice_in_dim(values, width, count, axis=axis), blank], axis=axis)


def block_gram(former, latter):
    return jnp.einsum("sxl,txl->st", former, latter, precision=HIGH)


def mix_block(values, matrix):
    return jnp.einsum("ts,sxl->txl", matrix.T, values, precision=HIGH)


def chol_factor(gram_mat):
    low_factor = jnp.linalg.cholesky(gram_mat)
    eye_mat = jnp.eye(gram_mat.shape[0], dtype=gram_mat.dtype)
    inverse = lax.linalg.triangular_solve(low_factor, eye_mat, left_side=True, lower=True)
    return (low_factor.T, inverse.T)


def solve_small(columns, first_factor):
    hessen = jnp.concatenate(columns, axis=1)
    count_rhs = first_factor.shape[0]
    target = jnp.dot(hessen[:count_rhs].T, first_factor, precision=HIGH)
    normal = jnp.dot(hessen.T, hessen, precision=HIGH)
    low_factor = jnp.linalg.cholesky(normal)
    partial_sol = lax.linalg.triangular_solve(low_factor, target, left_side=True, lower=True)
    return lax.linalg.triangular_solve(
        low_factor, partial_sol, left_side=True, lower=True, transpose_a=True
    )


def body(right_side, start_guess, couple_x, couple_y, couple_z, reaction):
    rows_x, rows_y, flat_len = right_side.shape
    layers = couple_z.shape[2]
    count_rhs = flat_len // layers
    plane = rows_y * layers
    depth = jnp.arange(plane, dtype=jnp.int32) % layers
    keep_first = (depth != 0).astype(jnp.float32)
    keep_last = (depth != layers - 1).astype(jnp.float32)

    def inward(values):
        split = values.reshape(rows_x, rows_y, count_rhs, layers)
        return jnp.transpose(split, (2, 0, 1, 3)).reshape(count_rhs, rows_x, plane)

    def outward(values):
        split = values.reshape(count_rhs, rows_x, rows_y, layers)
        return jnp.transpose(split, (1, 2, 0, 3)).reshape(rows_x, rows_y, flat_len)

    def coef(values):
        return values.reshape(1, rows_x, plane)

    def low_x(values):
        return low_along(values, 1, 1)

    def up_x(values):
        return up_along(values, 1, 1)

    def low_y(values):
        return low_along(values, 2, layers)

    def up_y(values):
        return up_along(values, 2, layers)

    def low_z(values):
        return low_along(values, 2, 1) * keep_first

    def up_z(values):
        return up_along(values, 2, 1) * keep_last

    def forward(block, axis):
        count = lax.axis_size(axis)
        return lax.ppermute(block, axis, [(i, i + 1) for i in range(count - 1)])

    def backward(block, axis):
        count = lax.axis_size(axis)
        return lax.ppermute(block, axis, [(i + 1, i) for i in range(count - 1)])

    after_x = coef(couple_x)
    after_y = coef(couple_y)
    after_z = coef(couple_z)
    edge_x = forward(after_x[:, -1:], "gx")
    edge_y = forward(after_y[:, :, plane - layers :], "gy")
    before_x = jnp.concatenate([edge_x, after_x[:, :-1]], axis=1)
    before_y = jnp.concatenate([edge_y, after_y[:, :, : plane - layers]], axis=2)
    before_z = low_z(after_z)
    diagonal = coef(reaction) + after_x + before_x + after_y + before_y + after_z + before_z

    def halos(values):
        return (
            forward(values[:, -1:], "gx"),
            backward(values[:, :1], "gx"),
            forward(values[:, :, plane - layers :], "gy"),
            backward(values[:, :, :layers], "gy"),
        )

    def apply_op(values, edges):
        from_low_x, from_high_x, from_low_y, from_high_y = edges
        next_x = jnp.concatenate([values[:, 1:], from_high_x], axis=1)
        prev_x = jnp.concatenate([from_low_x, values[:, :-1]], axis=1)
        next_y = jnp.concatenate([values[:, :, layers:], from_high_y], axis=2)
        prev_y = jnp.concatenate([from_low_y, values[:, :, : plane - layers]], axis=2)
        return (
            diagonal * values
            - after_x * next_x
            - before_x * prev_x
            - after_y * next_y
            - before_y * prev_y
            - after_z * up_z(values)
            - before_z * low_z(values)
        )

    lows = (low_x(after_x), low_y(after_y), before_z)
    ups = (
        up_x(jnp.ones_like(after_x)) * after_x,
        up_y(jnp.ones_like(after_y)) * after_y,
        after_z,
    )
    pivots = diagonal
    for repeat in range(FACT_SWEEPS):
        inv_now = 1.0 / pivots
        pivots = (
            diagonal
            - lows[0] * lows[0] * low_x(inv_now)
            - lows[1] * lows[1] * low_y(inv_now)
            - lows[2] * lows[2] * low_z(inv_now)
        )
    inv_piv = 1.0 / pivots

    def total_gram(former, latter):
        return mesh_sum(block_gram(former, latter))

    rhs_in = inward(right_side)
    start_in = inward(start_guess)
    def precondition(source):
        lower_sol = inv_piv * source
        for precondition_repeat in range(SWEEPS):
            lower_sol = inv_piv * (
                source
                + lows[0] * low_x(lower_sol)
                + lows[1] * low_y(lower_sol)
                + lows[2] * low_z(lower_sol)
            )
        upper_sol = lower_sol
        for precondition_repeat in range(SWEEPS):
            upper_sol = lower_sol + inv_piv * (
                ups[0] * up_x(upper_sol)
                + ups[1] * up_y(upper_sol)
                + ups[2] * up_z(upper_sol)
            )
        return upper_sol

    start_edges = halos(start_in)
    start_res = rhs_in - apply_op(start_in, start_edges)
    krylov = [start_res]
    precond_set = []
    applied_set = []
    for column in range(ITERS):
        turned = precondition(krylov[-1])
        turned_edges = halos(turned)
        precond_set.append(turned)
        applied_set.append(apply_op(turned, turned_edges))
        krylov.append(applied_set[-1] - SHIFT * krylov[-1])
    stacked = jnp.concatenate(krylov, axis=0)
    span_gram = mesh_sum(block_gram(stacked, stacked))
    width = span_gram.shape[0]

    def inner(left, right):
        return jnp.dot(left.T, jnp.dot(span_gram, right, precision=HIGH), precision=HIGH)

    def advance(weights):
        moved = jnp.concatenate([jnp.zeros_like(weights[:count_rhs]), weights[:-count_rhs]], axis=0)
        return moved + SHIFT * weights

    first_factor, first_inv = chol_factor(inner(*(2 * [jnp.eye(width, count_rhs, dtype=jnp.float32)])))
    basis_set = [jnp.dot(jnp.eye(width, count_rhs, dtype=jnp.float32), first_inv, precision=HIGH)]
    columns = []
    for column in range(ITERS):
        image = advance(basis_set[column])
        projections = [inner(member, image) for member in basis_set]
        perp = image - sum(
            jnp.dot(member, proj, precision=HIGH) for member, proj in zip(basis_set, projections)
        )
        next_factor, next_inv = chol_factor(inner(perp, perp))
        if column + 1 < ITERS:
            basis_set.append(jnp.dot(perp, next_inv, precision=HIGH))
        blank = jnp.zeros(((ITERS - 1 - column) * count_rhs, count_rhs), dtype=next_factor.dtype)
        columns.append(jnp.concatenate(projections + [next_factor, blank], axis=0))
    coeffs = solve_small(columns, first_factor)
    combined = sum(
        jnp.dot(basis_set[column], coeffs[column * count_rhs : (column + 1) * count_rhs], precision=HIGH)
        for column in range(ITERS)
    )
    solution = start_in
    residual = start_res
    for column in range(ITERS):
        weights = combined[column * count_rhs : (column + 1) * count_rhs]
        solution = solution + mix_block(precond_set[column], weights)
        residual = residual - mix_block(applied_set[column], weights)
    return (outward(solution), outward(residual))


def solution(mesh):
    return jax.shard_map(
        body,
        mesh=mesh,
        in_specs=(
            P("gx", "gy", None),
            P("gx", "gy", None),
            P("gx", "gy", None),
            P("gx", "gy", None),
            P("gx", "gy", None),
            P("gx", "gy", None),
        ),
        out_specs=(P("gx", "gy", None), P("gx", "gy", None)),
        check_vma=False,
    )
```

```python
import jax
import jax.numpy as jnp
from jax import lax
from jax.sharding import PartitionSpec as P

ITERS = 2
SWEEPS = 4
FACT_SWEEPS = 3
SHIFT = 1.0


HIGH = lax.Precision.HIGHEST


def mesh_sum(block):
    for axis in ("gx", "gy"):
        count = lax.axis_size(axis)
        if count & (count - 1):
            block = lax.psum(block, axis)
            continue
        step = 1
        while step < count:
            radix = 4 if count % (step * 4) == 0 else 2
            parts = [block] + [
                lax.ppermute(block, axis, [(i, i ^ (step * m)) for i in range(count)])
                for m in range(1, radix)
            ]
            while len(parts) > 1:
                parts = [parts[i] + parts[i + 1] for i in range(0, len(parts), 2)]
            block = parts[0]
            step *= radix
    return block


def low_along(values, axis, width):
    count = values.shape[axis]
    blank = jnp.zeros_like(lax.slice_in_dim(values, 0, width, axis=axis))
    return jnp.concatenate([blank, lax.slice_in_dim(values, 0, count - width, axis=axis)], axis=axis)


def up_along(values, axis, width):
    count = values.shape[axis]
    blank = jnp.zeros_like(lax.slice_in_dim(values, 0, width, axis=axis))
    return jnp.concatenate([lax.slice_in_dim(values, width, count, axis=axis), blank], axis=axis)


def block_gram(former, latter):
    return jnp.einsum("sxl,txl->st", former, latter, precision=HIGH)


def mix_block(values, matrix):
    return jnp.einsum("ts,sxl->txl", matrix.T, values, precision=HIGH)


def solve_small(columns, first_factor):
    hessen = jnp.concatenate(columns, axis=1)
    count_rhs = first_factor.shape[0]
    target = jnp.dot(hessen[:count_rhs].T, first_factor, precision=HIGH)
    normal = jnp.dot(hessen.T, hessen, precision=HIGH)
    low_factor = jnp.linalg.cholesky(normal)
    partial_sol = lax.linalg.triangular_solve(low_factor, target, left_side=True, lower=True)
    return lax.linalg.triangular_solve(
        low_factor, partial_sol, left_side=True, lower=True, transpose_a=True
    )


def body(right_side, start_guess, couple_x, couple_y, couple_z, reaction):
    rows_x, rows_y, flat_len = right_side.shape
    layers = couple_z.shape[2]
    count_rhs = flat_len // layers
    plane = rows_y * layers
    depth = jnp.arange(plane, dtype=jnp.int32) % layers
    keep_first = (depth != 0).astype(jnp.float32)
    keep_last = (depth != layers - 1).astype(jnp.float32)

    def inward(values):
        split = values.reshape(rows_x, rows_y, count_rhs, layers)
        return jnp.transpose(split, (2, 0, 1, 3)).reshape(count_rhs, rows_x, plane)

    def outward(values):
        split = values.reshape(count_rhs, rows_x, rows_y, layers)
        return jnp.transpose(split, (1, 2, 0, 3)).reshape(rows_x, rows_y, flat_len)

    def coef(values):
        return values.reshape(1, rows_x, plane)

    def low_x(values):
        return low_along(values, 1, 1)

    def up_x(values):
        return up_along(values, 1, 1)

    def low_y(values):
        return low_along(values, 2, layers)

    def up_y(values):
        return up_along(values, 2, layers)

    def low_z(values):
        return low_along(values, 2, 1) * keep_first

    def up_z(values):
        return up_along(values, 2, 1) * keep_last

    def forward(block, axis):
        count = lax.axis_size(axis)
        return lax.ppermute(block, axis, [(i, i + 1) for i in range(count - 1)])

    def backward(block, axis):
        count = lax.axis_size(axis)
        return lax.ppermute(block, axis, [(i + 1, i) for i in range(count - 1)])

    after_x = coef(couple_x)
    after_y = coef(couple_y)
    after_z = coef(couple_z)
    edge_x = forward(after_x[:, -1:], "gx")
    edge_y = forward(after_y[:, :, plane - layers :], "gy")
    before_x = jnp.concatenate([edge_x, after_x[:, :-1]], axis=1)
    before_y = jnp.concatenate([edge_y, after_y[:, :, : plane - layers]], axis=2)
    before_z = low_z(after_z)
    diagonal = coef(reaction) + after_x + before_x + after_y + before_y + after_z + before_z

    def halos(values):
        return (
            forward(values[:, -1:], "gx"),
            backward(values[:, :1], "gx"),
            forward(values[:, :, plane - layers :], "gy"),
            backward(values[:, :, :layers], "gy"),
        )

    def apply_op(values, edges):
        from_low_x, from_high_x, from_low_y, from_high_y = edges
        next_x = jnp.concatenate([values[:, 1:], from_high_x], axis=1)
        prev_x = jnp.concatenate([from_low_x, values[:, :-1]], axis=1)
        next_y = jnp.concatenate([values[:, :, layers:], from_high_y], axis=2)
        prev_y = jnp.concatenate([from_low_y, values[:, :, : plane - layers]], axis=2)
        return (
            diagonal * values
            - after_x * next_x
            - before_x * prev_x
            - after_y * next_y
            - before_y * prev_y
            - after_z * up_z(values)
            - before_z * low_z(values)
        )

    lows = (low_x(after_x), low_y(after_y), before_z)
    ups = (
        up_x(jnp.ones_like(after_x)) * after_x,
        up_y(jnp.ones_like(after_y)) * after_y,
        after_z,
    )
    pivots = diagonal
    for repeat in range(FACT_SWEEPS):
        inv_now = 1.0 / pivots
        pivots = (
            diagonal
            - lows[0] * lows[0] * low_x(inv_now)
            - lows[1] * lows[1] * low_y(inv_now)
            - lows[2] * lows[2] * low_z(inv_now)
        )
    inv_piv = 1.0 / pivots

    def total_gram(former, latter):
        return mesh_sum(block_gram(former, latter))

    rhs_in = inward(right_side)
    start_in = inward(start_guess)
    def precondition(source):
        lower_sol = inv_piv * source
        for precondition_repeat in range(SWEEPS):
            lower_sol = inv_piv * (
                source
                + lows[0] * low_x(lower_sol)
                + lows[1] * low_y(lower_sol)
                + lows[2] * low_z(lower_sol)
            )
        upper_sol = lower_sol
        for precondition_repeat in range(SWEEPS):
            upper_sol = lower_sol + inv_piv * (
                ups[0] * up_x(upper_sol)
                + ups[1] * up_y(upper_sol)
                + ups[2] * up_z(upper_sol)
            )
        return upper_sol

    start_edges = halos(start_in)
    start_res = rhs_in - apply_op(start_in, start_edges)
    krylov = [start_res]
    precond_set = []
    applied_set = []
    for column in range(ITERS):
        turned = precondition(krylov[-1])
        turned_edges = halos(turned)
        precond_set.append(turned)
        applied_set.append(apply_op(turned, turned_edges))
        krylov.append(applied_set[-1] - SHIFT * krylov[-1])
    stacked = jnp.concatenate(krylov, axis=0)
    span_gram = mesh_sum(block_gram(stacked, stacked))
    width = span_gram.shape[0]

    full_low = jnp.linalg.cholesky(span_gram)
    upper = full_low.T
    head = ITERS * count_rhs
    head_inv = lax.linalg.triangular_solve(
        full_low[:head, :head], jnp.eye(head, dtype=jnp.float32), left_side=True, lower=True
    ).T
    advance = jnp.eye(width, head, k=-count_rhs, dtype=jnp.float32) + SHIFT * jnp.eye(width, head, dtype=jnp.float32)
    hessen = jnp.dot(jnp.dot(upper, advance, precision=HIGH), head_inv, precision=HIGH)
    first_factor = upper[:count_rhs, :count_rhs]
    coeffs = solve_small([hessen], first_factor)
    combined = jnp.dot(head_inv, coeffs, precision=HIGH)
    solution = start_in
    residual = start_res
    for column in range(ITERS):
        weights = combined[column * count_rhs : (column + 1) * count_rhs]
        solution = solution + mix_block(precond_set[column], weights)
        residual = residual - mix_block(applied_set[column], weights)
    return (outward(solution), outward(residual))


def solution(mesh):
    return jax.shard_map(
        body,
        mesh=mesh,
        in_specs=(
            P("gx", "gy", None),
            P("gx", "gy", None),
            P("gx", "gy", None),
            P("gx", "gy", None),
            P("gx", "gy", None),
            P("gx", "gy", None),
        ),
        out_specs=(P("gx", "gy", None), P("gx", "gy", None)),
        check_vma=False,
    )
```

```python
import jax
import jax.numpy as jnp
from jax import lax
from jax.sharding import PartitionSpec as P

ITERS = 2
SWEEPS = 4
FACT_SWEEPS = 3
SHIFT = 1.0


HIGH = lax.Precision.HIGHEST


def mesh_sum(block):
    for axis in ("gx", "gy"):
        count = lax.axis_size(axis)
        if count & (count - 1):
            block = lax.psum(block, axis)
            continue
        step = 1
        while step < count:
            radix = 4 if count % (step * 4) == 0 else 2
            parts = [block] + [
                lax.ppermute(block, axis, [(i, i ^ (step * m)) for i in range(count)])
                for m in range(1, radix)
            ]
            while len(parts) > 1:
                parts = [parts[i] + parts[i + 1] for i in range(0, len(parts), 2)]
            block = parts[0]
            step *= radix
    return block


def low_along(values, axis, width):
    count = values.shape[axis]
    blank = jnp.zeros_like(lax.slice_in_dim(values, 0, width, axis=axis))
    return jnp.concatenate([blank, lax.slice_in_dim(values, 0, count - width, axis=axis)], axis=axis)


def up_along(values, axis, width):
    count = values.shape[axis]
    blank = jnp.zeros_like(lax.slice_in_dim(values, 0, width, axis=axis))
    return jnp.concatenate([lax.slice_in_dim(values, width, count, axis=axis), blank], axis=axis)


def block_gram(former, latter):
    return jnp.einsum("sxl,txl->st", former, latter, precision=HIGH)


def mix_block(values, matrix):
    return jnp.einsum("ts,sxl->txl", matrix.T, values, precision=HIGH)


def solve_small(columns, first_factor):
    hessen = jnp.concatenate(columns, axis=1)
    count_rhs = first_factor.shape[0]
    target = jnp.dot(hessen[:count_rhs].T, first_factor, precision=HIGH)
    normal = jnp.dot(hessen.T, hessen, precision=HIGH)
    low_factor = jnp.linalg.cholesky(normal)
    partial_sol = lax.linalg.triangular_solve(low_factor, target, left_side=True, lower=True)
    return lax.linalg.triangular_solve(
        low_factor, partial_sol, left_side=True, lower=True, transpose_a=True
    )


def body(right_side, start_guess, couple_x, couple_y, couple_z, reaction):
    rows_x, rows_y, flat_len = right_side.shape
    layers = couple_z.shape[2]
    count_rhs = flat_len // layers
    plane = rows_y * layers
    depth = jnp.arange(plane, dtype=jnp.int32) % layers
    keep_first = (depth != 0).astype(jnp.float32)
    keep_last = (depth != layers - 1).astype(jnp.float32)

    def inward(values):
        split = values.reshape(rows_x, rows_y, count_rhs, layers)
        return jnp.transpose(split, (2, 0, 1, 3)).reshape(count_rhs, rows_x, plane)

    def outward(values):
        split = values.reshape(count_rhs, rows_x, rows_y, layers)
        return jnp.transpose(split, (1, 2, 0, 3)).reshape(rows_x, rows_y, flat_len)

    def coef(values):
        return values.reshape(1, rows_x, plane)

    def low_x(values):
        return low_along(values, 1, 1)

    def up_x(values):
        return up_along(values, 1, 1)

    def low_y(values):
        return low_along(values, 2, layers)

    def up_y(values):
        return up_along(values, 2, layers)

    def low_z(values):
        return low_along(values, 2, 1) * keep_first

    def up_z(values):
        return up_along(values, 2, 1) * keep_last

    def forward(block, axis):
        count = lax.axis_size(axis)
        return lax.ppermute(block, axis, [(i, i + 1) for i in range(count - 1)])

    def backward(block, axis):
        count = lax.axis_size(axis)
        return lax.ppermute(block, axis, [(i + 1, i) for i in range(count - 1)])

    after_x = coef(couple_x)
    after_y = coef(couple_y)
    after_z = coef(couple_z)
    rhs_in = inward(right_side)
    start_in = inward(start_guess)
    joint_x = forward(jnp.concatenate([start_in[:, -1:], after_x[:, -1:]], axis=0), "gx")
    joint_y = forward(
        jnp.concatenate([start_in[:, :, plane - layers :], after_y[:, :, plane - layers :]], axis=0), "gy"
    )
    edge_x = joint_x[count_rhs:]
    edge_y = joint_y[count_rhs:]
    before_x = jnp.concatenate([edge_x, after_x[:, :-1]], axis=1)
    before_y = jnp.concatenate([edge_y, after_y[:, :, : plane - layers]], axis=2)
    before_z = low_z(after_z)
    diagonal = coef(reaction) + after_x + before_x + after_y + before_y + after_z + before_z

    def halos(values):
        return (
            forward(values[:, -1:], "gx"),
            backward(values[:, :1], "gx"),
            forward(values[:, :, plane - layers :], "gy"),
            backward(values[:, :, :layers], "gy"),
        )

    def apply_op(values, edges):
        from_low_x, from_high_x, from_low_y, from_high_y = edges
        next_x = jnp.concatenate([values[:, 1:], from_high_x], axis=1)
        prev_x = jnp.concatenate([from_low_x, values[:, :-1]], axis=1)
        next_y = jnp.concatenate([values[:, :, layers:], from_high_y], axis=2)
        prev_y = jnp.concatenate([from_low_y, values[:, :, : plane - layers]], axis=2)
        return (
            diagonal * values
            - after_x * next_x
            - before_x * prev_x
            - after_y * next_y
            - before_y * prev_y
            - after_z * up_z(values)
            - before_z * low_z(values)
        )

    lows = (low_x(after_x), low_y(after_y), before_z)
    ups = (
        up_x(jnp.ones_like(after_x)) * after_x,
        up_y(jnp.ones_like(after_y)) * after_y,
        after_z,
    )
    pivots = diagonal
    for repeat in range(FACT_SWEEPS):
        inv_now = 1.0 / pivots
        pivots = (
            diagonal
            - lows[0] * lows[0] * low_x(inv_now)
            - lows[1] * lows[1] * low_y(inv_now)
            - lows[2] * lows[2] * low_z(inv_now)
        )
    inv_piv = 1.0 / pivots

    def total_gram(former, latter):
        return mesh_sum(block_gram(former, latter))

    def precondition(source):
        lower_sol = inv_piv * source
        for precondition_repeat in range(SWEEPS):
            lower_sol = inv_piv * (
                source
                + lows[0] * low_x(lower_sol)
                + lows[1] * low_y(lower_sol)
                + lows[2] * low_z(lower_sol)
            )
        upper_sol = lower_sol
        for precondition_repeat in range(SWEEPS):
            upper_sol = lower_sol + inv_piv * (
                ups[0] * up_x(upper_sol)
                + ups[1] * up_y(upper_sol)
                + ups[2] * up_z(upper_sol)
            )
        return upper_sol

    start_edges = (
        joint_x[:count_rhs],
        backward(start_in[:, :1], "gx"),
        joint_y[:count_rhs],
        backward(start_in[:, :, :layers], "gy"),
    )
    start_res = rhs_in - apply_op(start_in, start_edges)
    krylov = [start_res]
    precond_set = []
    applied_set = []
    for column in range(ITERS):
        turned = precondition(krylov[-1])
        turned_edges = halos(turned)
        precond_set.append(turned)
        applied_set.append(apply_op(turned, turned_edges))
        krylov.append(applied_set[-1] - SHIFT * krylov[-1])
    stacked = jnp.concatenate(krylov, axis=0)
    span_gram = mesh_sum(block_gram(stacked, stacked))
    width = span_gram.shape[0]

    full_low = jnp.linalg.cholesky(span_gram)
    upper = full_low.T
    head = ITERS * count_rhs
    head_inv = lax.linalg.triangular_solve(
        full_low[:head, :head], jnp.eye(head, dtype=jnp.float32), left_side=True, lower=True
    ).T
    advance = jnp.eye(width, head, k=-count_rhs, dtype=jnp.float32) + SHIFT * jnp.eye(width, head, dtype=jnp.float32)
    hessen = jnp.dot(jnp.dot(upper, advance, precision=HIGH), head_inv, precision=HIGH)
    first_factor = upper[:count_rhs, :count_rhs]
    coeffs = solve_small([hessen], first_factor)
    combined = jnp.dot(head_inv, coeffs, precision=HIGH)
    solution = start_in
    residual = start_res
    for column in range(ITERS):
        weights = combined[column * count_rhs : (column + 1) * count_rhs]
        solution = solution + mix_block(precond_set[column], weights)
        residual = residual - mix_block(applied_set[column], weights)
    return (outward(solution), outward(residual))


def solution(mesh):
    return jax.shard_map(
        body,
        mesh=mesh,
        in_specs=(
            P("gx", "gy", None),
            P("gx", "gy", None),
            P("gx", "gy", None),
            P("gx", "gy", None),
            P("gx", "gy", None),
            P("gx", "gy", None),
        ),
        out_specs=(P("gx", "gy", None), P("gx", "gy", None)),
        check_vma=False,
    )
```

```python
import jax
import jax.numpy as jnp
from jax import lax
from jax.sharding import PartitionSpec as P

ITERS = 2
SWEEPS = 4
FACT_SWEEPS = 3
SHIFT = 1.0


HIGH = lax.Precision.HIGHEST


def mesh_sum(block):
    for axis in ("gx", "gy"):
        count = lax.axis_size(axis)
        if count & (count - 1):
            block = lax.psum(block, axis)
            continue
        step = 1
        while step < count:
            radix = 4 if count % (step * 4) == 0 else 2
            parts = [block] + [
                lax.ppermute(block, axis, [(i, i ^ (step * m)) for i in range(count)])
                for m in range(1, radix)
            ]
            while len(parts) > 1:
                parts = [parts[i] + parts[i + 1] for i in range(0, len(parts), 2)]
            block = parts[0]
            step *= radix
    return block


def low_along(values, axis, width):
    count = values.shape[axis]
    blank = jnp.zeros_like(lax.slice_in_dim(values, 0, width, axis=axis))
    return jnp.concatenate([blank, lax.slice_in_dim(values, 0, count - width, axis=axis)], axis=axis)


def up_along(values, axis, width):
    count = values.shape[axis]
    blank = jnp.zeros_like(lax.slice_in_dim(values, 0, width, axis=axis))
    return jnp.concatenate([lax.slice_in_dim(values, width, count, axis=axis), blank], axis=axis)


def block_gram(former, latter):
    return jnp.einsum("sxl,txl->st", former, latter, precision=HIGH)


def mix_block(values, matrix):
    return jnp.einsum("ts,sxl->txl", matrix.T, values, precision=HIGH)


def solve_small(columns, first_factor):
    hessen = jnp.concatenate(columns, axis=1)
    count_rhs = first_factor.shape[0]
    target = jnp.dot(hessen[:count_rhs].T, first_factor, precision=HIGH)
    normal = jnp.dot(hessen.T, hessen, precision=HIGH)
    low_factor = jnp.linalg.cholesky(normal)
    partial_sol = lax.linalg.triangular_solve(low_factor, target, left_side=True, lower=True)
    return lax.linalg.triangular_solve(
        low_factor, partial_sol, left_side=True, lower=True, transpose_a=True
    )


def body(right_side, start_guess, couple_x, couple_y, couple_z, reaction):
    rows_x, rows_y, flat_len = right_side.shape
    layers = couple_z.shape[2]
    count_rhs = flat_len // layers
    plane = rows_y * layers
    depth = jnp.arange(plane, dtype=jnp.int32) % layers
    keep_first = (depth != 0).astype(jnp.float32)
    keep_last = (depth != layers - 1).astype(jnp.float32)

    def inward(values):
        split = values.reshape(rows_x, rows_y, count_rhs, layers)
        return jnp.transpose(split, (2, 0, 1, 3)).reshape(count_rhs, rows_x, plane)

    def outward(values):
        split = values.reshape(count_rhs, rows_x, rows_y, layers)
        return jnp.transpose(split, (1, 2, 0, 3)).reshape(rows_x, rows_y, flat_len)

    def coef(values):
        return values.reshape(1, rows_x, plane)

    def low_x(values):
        return low_along(values, 1, 1)

    def up_x(values):
        return up_along(values, 1, 1)

    def low_y(values):
        return low_along(values, 2, layers)

    def up_y(values):
        return up_along(values, 2, layers)

    def low_z(values):
        return low_along(values, 2, 1) * keep_first

    def up_z(values):
        return up_along(values, 2, 1) * keep_last

    def forward(block, axis):
        count = lax.axis_size(axis)
        return lax.ppermute(block, axis, [(i, i + 1) for i in range(count - 1)])

    def backward(block, axis):
        count = lax.axis_size(axis)
        return lax.ppermute(block, axis, [(i + 1, i) for i in range(count - 1)])

    after_x = coef(couple_x)
    after_y = coef(couple_y)
    after_z = coef(couple_z)
    rhs_in = inward(right_side)
    start_in = inward(start_guess)

    def slab_in(values):
        count_a, count_b = values.shape[:2]
        split = values.reshape(count_a, count_b, count_rhs, layers)
        return jnp.transpose(split, (2, 0, 1, 3)).reshape(count_rhs, count_a, count_b * layers)

    joint_x = forward(jnp.concatenate([start_guess[-1:], couple_x[-1:]], axis=2), "gx")
    joint_y = forward(jnp.concatenate([start_guess[:, -1:], couple_y[:, -1:]], axis=2), "gy")
    edge_x = joint_x[:, :, flat_len:].reshape(1, 1, plane)
    edge_y = joint_y[:, :, flat_len:].reshape(1, rows_x, layers)
    before_x = jnp.concatenate([edge_x, after_x[:, :-1]], axis=1)
    before_y = jnp.concatenate([edge_y, after_y[:, :, : plane - layers]], axis=2)
    before_z = low_z(after_z)
    diagonal = coef(reaction) + after_x + before_x + after_y + before_y + after_z + before_z

    def halos(values):
        return (
            forward(values[:, -1:], "gx"),
            backward(values[:, :1], "gx"),
            forward(values[:, :, plane - layers :], "gy"),
            backward(values[:, :, :layers], "gy"),
        )

    def apply_op(values, edges):
        from_low_x, from_high_x, from_low_y, from_high_y = edges
        next_x = jnp.concatenate([values[:, 1:], from_high_x], axis=1)
        prev_x = jnp.concatenate([from_low_x, values[:, :-1]], axis=1)
        next_y = jnp.concatenate([values[:, :, layers:], from_high_y], axis=2)
        prev_y = jnp.concatenate([from_low_y, values[:, :, : plane - layers]], axis=2)
        return (
            diagonal * values
            - after_x * next_x
            - before_x * prev_x
            - after_y * next_y
            - before_y * prev_y
            - after_z * up_z(values)
            - before_z * low_z(values)
        )

    lows = (low_x(after_x), low_y(after_y), before_z)
    ups = (
        up_x(jnp.ones_like(after_x)) * after_x,
        up_y(jnp.ones_like(after_y)) * after_y,
        after_z,
    )
    pivots = diagonal
    for repeat in range(FACT_SWEEPS):
        inv_now = 1.0 / pivots
        pivots = (
            diagonal
            - lows[0] * lows[0] * low_x(inv_now)
            - lows[1] * lows[1] * low_y(inv_now)
            - lows[2] * lows[2] * low_z(inv_now)
        )
    inv_piv = 1.0 / pivots

    def total_gram(former, latter):
        return mesh_sum(block_gram(former, latter))

    def precondition(source):
        lower_sol = inv_piv * source
        for precondition_repeat in range(SWEEPS):
            lower_sol = inv_piv * (
                source
                + lows[0] * low_x(lower_sol)
                + lows[1] * low_y(lower_sol)
                + lows[2] * low_z(lower_sol)
            )
        upper_sol = lower_sol
        for precondition_repeat in range(SWEEPS):
            upper_sol = lower_sol + inv_piv * (
                ups[0] * up_x(upper_sol)
                + ups[1] * up_y(upper_sol)
                + ups[2] * up_z(upper_sol)
            )
        return upper_sol

    start_edges = (
        slab_in(joint_x[:, :, :flat_len]),
        slab_in(backward(start_guess[:1], "gx")),
        slab_in(joint_y[:, :, :flat_len]).reshape(count_rhs, rows_x, layers),
        slab_in(backward(start_guess[:, :1], "gy")).reshape(count_rhs, rows_x, layers),
    )
    start_res = rhs_in - apply_op(start_in, start_edges)
    krylov = [start_res]
    precond_set = []
    applied_set = []
    for column in range(ITERS):
        turned = precondition(krylov[-1])
        turned_edges = halos(turned)
        precond_set.append(turned)
        applied_set.append(apply_op(turned, turned_edges))
        krylov.append(applied_set[-1] - SHIFT * krylov[-1])
    stacked = jnp.concatenate(krylov, axis=0)
    span_gram = mesh_sum(block_gram(stacked, stacked))
    width = span_gram.shape[0]

    full_low = jnp.linalg.cholesky(span_gram)
    upper = full_low.T
    head = ITERS * count_rhs
    head_inv = lax.linalg.triangular_solve(
        full_low[:head, :head], jnp.eye(head, dtype=jnp.float32), left_side=True, lower=True
    ).T
    advance = jnp.eye(width, head, k=-count_rhs, dtype=jnp.float32) + SHIFT * jnp.eye(width, head, dtype=jnp.float32)
    hessen = jnp.dot(jnp.dot(upper, advance, precision=HIGH), head_inv, precision=HIGH)
    first_factor = upper[:count_rhs, :count_rhs]
    coeffs = solve_small([hessen], first_factor)
    combined = jnp.dot(head_inv, coeffs, precision=HIGH)
    solution = start_in
    residual = start_res
    for column in range(ITERS):
        weights = combined[column * count_rhs : (column + 1) * count_rhs]
        solution = solution + mix_block(precond_set[column], weights)
        residual = residual - mix_block(applied_set[column], weights)
    return (outward(solution), outward(residual))


def solution(mesh):
    return jax.shard_map(
        body,
        mesh=mesh,
        in_specs=(
            P("gx", "gy", None),
            P("gx", "gy", None),
            P("gx", "gy", None),
            P("gx", "gy", None),
            P("gx", "gy", None),
            P("gx", "gy", None),
        ),
        out_specs=(P("gx", "gy", None), P("gx", "gy", None)),
        check_vma=False,
    )
```

```python
import jax
import jax.numpy as jnp
from jax import lax
from jax.sharding import PartitionSpec as P

ITERS = 2
SWEEPS = 4
FACT_SWEEPS = 3
SHIFT = 1.0


HIGH = lax.Precision.HIGHEST


def mesh_sum(block):
    for axis in ("gy", "gx"):
        count = lax.axis_size(axis)
        if count & (count - 1):
            block = lax.psum(block, axis)
            continue
        step = 1
        while step < count:
            radix = 4 if count % (step * 4) == 0 else 2
            parts = [block] + [
                lax.ppermute(block, axis, [(i, i ^ (step * m)) for i in range(count)])
                for m in range(1, radix)
            ]
            while len(parts) > 1:
                parts = [parts[i] + parts[i + 1] for i in range(0, len(parts), 2)]
            block = parts[0]
            step *= radix
    return block


def low_along(values, axis, width):
    count = values.shape[axis]
    blank = jnp.zeros_like(lax.slice_in_dim(values, 0, width, axis=axis))
    return jnp.concatenate([blank, lax.slice_in_dim(values, 0, count - width, axis=axis)], axis=axis)


def up_along(values, axis, width):
    count = values.shape[axis]
    blank = jnp.zeros_like(lax.slice_in_dim(values, 0, width, axis=axis))
    return jnp.concatenate([lax.slice_in_dim(values, width, count, axis=axis), blank], axis=axis)


def block_gram(former, latter):
    return jnp.einsum("sxl,txl->st", former, latter, precision=HIGH)


def mix_block(values, matrix):
    return jnp.einsum("ts,sxl->txl", matrix.T, values, precision=HIGH)


def solve_small(columns, first_factor):
    hessen = jnp.concatenate(columns, axis=1)
    count_rhs = first_factor.shape[0]
    target = jnp.dot(hessen[:count_rhs].T, first_factor, precision=HIGH)
    normal = jnp.dot(hessen.T, hessen, precision=HIGH)
    low_factor = jnp.linalg.cholesky(normal)
    partial_sol = lax.linalg.triangular_solve(low_factor, target, left_side=True, lower=True)
    return lax.linalg.triangular_solve(
        low_factor, partial_sol, left_side=True, lower=True, transpose_a=True
    )


def body(right_side, start_guess, couple_x, couple_y, couple_z, reaction):
    rows_x, rows_y, flat_len = right_side.shape
    layers = couple_z.shape[2]
    count_rhs = flat_len // layers
    plane = rows_y * layers
    depth = jnp.arange(plane, dtype=jnp.int32) % layers
    keep_first = (depth != 0).astype(jnp.float32)
    keep_last = (depth != layers - 1).astype(jnp.float32)

    def inward(values):
        split = values.reshape(rows_x, rows_y, count_rhs, layers)
        return jnp.transpose(split, (2, 0, 1, 3)).reshape(count_rhs, rows_x, plane)

    def outward(values):
        split = values.reshape(count_rhs, rows_x, rows_y, layers)
        return jnp.transpose(split, (1, 2, 0, 3)).reshape(rows_x, rows_y, flat_len)

    def coef(values):
        return values.reshape(1, rows_x, plane)

    def low_x(values):
        return low_along(values, 1, 1)

    def up_x(values):
        return up_along(values, 1, 1)

    def low_y(values):
        return low_along(values, 2, layers)

    def up_y(values):
        return up_along(values, 2, layers)

    def low_z(values):
        return low_along(values, 2, 1) * keep_first

    def up_z(values):
        return up_along(values, 2, 1) * keep_last

    def forward(block, axis):
        count = lax.axis_size(axis)
        return lax.ppermute(block, axis, [(i, i + 1) for i in range(count - 1)])

    def backward(block, axis):
        count = lax.axis_size(axis)
        return lax.ppermute(block, axis, [(i + 1, i) for i in range(count - 1)])

    after_x = coef(couple_x)
    after_y = coef(couple_y)
    after_z = coef(couple_z)
    rhs_in = inward(right_side)
    start_in = inward(start_guess)
    joint_x = forward(jnp.concatenate([start_in[:, -1:], after_x[:, -1:]], axis=0), "gx")
    joint_y = forward(
        jnp.concatenate([start_in[:, :, plane - layers :], after_y[:, :, plane - layers :]], axis=0), "gy"
    )
    edge_x = joint_x[count_rhs:]
    edge_y = joint_y[count_rhs:]
    before_x = jnp.concatenate([edge_x, after_x[:, :-1]], axis=1)
    before_y = jnp.concatenate([edge_y, after_y[:, :, : plane - layers]], axis=2)
    before_z = low_z(after_z)
    diagonal = coef(reaction) + after_x + before_x + after_y + before_y + after_z + before_z

    def halos(values):
        return (
            forward(values[:, -1:], "gx"),
            backward(values[:, :1], "gx"),
            forward(values[:, :, plane - layers :], "gy"),
            backward(values[:, :, :layers], "gy"),
        )

    def apply_op(values, edges):
        from_low_x, from_high_x, from_low_y, from_high_y = edges
        next_x = jnp.concatenate([values[:, 1:], from_high_x], axis=1)
        prev_x = jnp.concatenate([from_low_x, values[:, :-1]], axis=1)
        next_y = jnp.concatenate([values[:, :, layers:], from_high_y], axis=2)
        prev_y = jnp.concatenate([from_low_y, values[:, :, : plane - layers]], axis=2)
        return (
            diagonal * values
            - after_x * next_x
            - before_x * prev_x
            - after_y * next_y
            - before_y * prev_y
            - after_z * up_z(values)
            - before_z * low_z(values)
        )

    lows = (low_x(after_x), low_y(after_y), before_z)
    ups = (
        up_x(jnp.ones_like(after_x)) * after_x,
        up_y(jnp.ones_like(after_y)) * after_y,
        after_z,
    )
    pivots = diagonal
    for repeat in range(FACT_SWEEPS):
        inv_now = 1.0 / pivots
        pivots = (
            diagonal
            - lows[0] * lows[0] * low_x(inv_now)
            - lows[1] * lows[1] * low_y(inv_now)
            - lows[2] * lows[2] * low_z(inv_now)
        )
    inv_piv = 1.0 / pivots

    def total_gram(former, latter):
        return mesh_sum(block_gram(former, latter))

    def precondition(source):
        lower_sol = inv_piv * source
        for precondition_repeat in range(SWEEPS):
            lower_sol = inv_piv * (
                source
                + lows[0] * low_x(lower_sol)
                + lows[1] * low_y(lower_sol)
                + lows[2] * low_z(lower_sol)
            )
        upper_sol = lower_sol
        for precondition_repeat in range(SWEEPS):
            upper_sol = lower_sol + inv_piv * (
                ups[0] * up_x(upper_sol)
                + ups[1] * up_y(upper_sol)
                + ups[2] * up_z(upper_sol)
            )
        return upper_sol

    start_edges = (
        joint_x[:count_rhs],
        backward(start_in[:, :1], "gx"),
        joint_y[:count_rhs],
        backward(start_in[:, :, :layers], "gy"),
    )
    start_res = rhs_in - apply_op(start_in, start_edges)
    krylov = [start_res]
    precond_set = []
    applied_set = []
    for column in range(ITERS):
        turned = precondition(krylov[-1])
        turned_edges = halos(turned)
        precond_set.append(turned)
        applied_set.append(apply_op(turned, turned_edges))
        krylov.append(applied_set[-1] - SHIFT * krylov[-1])
    stacked = jnp.concatenate(krylov, axis=0)
    span_gram = mesh_sum(block_gram(stacked, stacked))
    width = span_gram.shape[0]

    full_low = jnp.linalg.cholesky(span_gram)
    upper = full_low.T
    head = ITERS * count_rhs
    head_inv = lax.linalg.triangular_solve(
        full_low[:head, :head], jnp.eye(head, dtype=jnp.float32), left_side=True, lower=True
    ).T
    advance = jnp.eye(width, head, k=-count_rhs, dtype=jnp.float32) + SHIFT * jnp.eye(width, head, dtype=jnp.float32)
    hessen = jnp.dot(jnp.dot(upper, advance, precision=HIGH), head_inv, precision=HIGH)
    first_factor = upper[:count_rhs, :count_rhs]
    coeffs = solve_small([hessen], first_factor)
    combined = jnp.dot(head_inv, coeffs, precision=HIGH)
    solution = start_in
    residual = start_res
    for column in range(ITERS):
        weights = combined[column * count_rhs : (column + 1) * count_rhs]
        solution = solution + mix_block(precond_set[column], weights)
        residual = residual - mix_block(applied_set[column], weights)
    return (outward(solution), outward(residual))


def solution(mesh):
    return jax.shard_map(
        body,
        mesh=mesh,
        in_specs=(
            P("gx", "gy", None),
            P("gx", "gy", None),
            P("gx", "gy", None),
            P("gx", "gy", None),
            P("gx", "gy", None),
            P("gx", "gy", None),
        ),
        out_specs=(P("gx", "gy", None), P("gx", "gy", None)),
        check_vma=False,
    )
```

```python
import jax
import jax.numpy as jnp
from jax import lax
from jax.sharding import PartitionSpec as P

ITERS = 2
SWEEPS = 4
FACT_SWEEPS = 3
SHIFT = 1.0


HIGH = lax.Precision.HIGHEST


def mesh_sum(block):
    for axis in ("gx", "gy"):
        count = lax.axis_size(axis)
        if count & (count - 1):
            block = lax.psum(block, axis)
            continue
        step = 1
        while step < count:
            radix = 4 if count % (step * 4) == 0 else 2
            parts = [block] + [
                lax.ppermute(block, axis, [(i, i ^ (step * m)) for i in range(count)])
                for m in range(1, radix)
            ]
            while len(parts) > 1:
                parts = [parts[i] + parts[i + 1] for i in range(0, len(parts), 2)]
            block = parts[0]
            step *= radix
    return block


def low_along(values, axis, width):
    count = values.shape[axis]
    blank = jnp.zeros_like(lax.slice_in_dim(values, 0, width, axis=axis))
    return jnp.concatenate([blank, lax.slice_in_dim(values, 0, count - width, axis=axis)], axis=axis)


def up_along(values, axis, width):
    count = values.shape[axis]
    blank = jnp.zeros_like(lax.slice_in_dim(values, 0, width, axis=axis))
    return jnp.concatenate([lax.slice_in_dim(values, width, count, axis=axis), blank], axis=axis)


def block_gram(former, latter):
    return jnp.einsum("sxl,txl->st", former, latter, precision=HIGH)


def mix_block(values, matrix):
    return jnp.einsum("ts,sxl->txl", matrix.T, values, precision=HIGH)


def solve_small(columns, first_factor):
    hessen = jnp.concatenate(columns, axis=1)
    count_rhs = first_factor.shape[0]
    target = jnp.dot(hessen[:count_rhs].T, first_factor, precision=HIGH)
    normal = jnp.dot(hessen.T, hessen, precision=HIGH)
    low_factor = jnp.linalg.cholesky(normal)
    partial_sol = lax.linalg.triangular_solve(low_factor, target, left_side=True, lower=True)
    return lax.linalg.triangular_solve(
        low_factor, partial_sol, left_side=True, lower=True, transpose_a=True
    )


def body(right_side, start_guess, couple_x, couple_y, couple_z, reaction):
    rows_x, rows_y, flat_len = right_side.shape
    layers = couple_z.shape[2]
    count_rhs = flat_len // layers
    plane = rows_y * layers
    depth = jnp.arange(plane, dtype=jnp.int32) % layers
    keep_first = (depth != 0).astype(jnp.float32)
    keep_last = (depth != layers - 1).astype(jnp.float32)

    def inward(values):
        split = values.reshape(rows_x, rows_y, count_rhs, layers)
        return jnp.transpose(split, (2, 0, 1, 3)).reshape(count_rhs, rows_x, plane)

    def outward(values):
        split = values.reshape(count_rhs, rows_x, rows_y, layers)
        return jnp.transpose(split, (1, 2, 0, 3)).reshape(rows_x, rows_y, flat_len)

    def coef(values):
        return values.reshape(1, rows_x, plane)

    def low_x(values):
        return low_along(values, 1, 1)

    def up_x(values):
        return up_along(values, 1, 1)

    def low_y(values):
        return low_along(values, 2, layers)

    def up_y(values):
        return up_along(values, 2, layers)

    def low_z(values):
        return low_along(values, 2, 1) * keep_first

    def up_z(values):
        return up_along(values, 2, 1) * keep_last

    def forward(block, axis):
        count = lax.axis_size(axis)
        return lax.ppermute(block, axis, [(i, i + 1) for i in range(count - 1)])

    def backward(block, axis):
        count = lax.axis_size(axis)
        return lax.ppermute(block, axis, [(i + 1, i) for i in range(count - 1)])

    after_x = coef(couple_x)
    after_y = coef(couple_y)
    after_z = coef(couple_z)
    rhs_in = inward(right_side)
    start_in = inward(start_guess)
    joint_x = forward(jnp.concatenate([start_in[:, -1:], after_x[:, -1:]], axis=0), "gx")
    joint_y = forward(
        jnp.concatenate([start_in[:, :, plane - layers :], after_y[:, :, plane - layers :]], axis=0), "gy"
    )
    edge_x = joint_x[count_rhs:]
    edge_y = joint_y[count_rhs:]
    before_x = jnp.concatenate([edge_x, after_x[:, :-1]], axis=1)
    before_y = jnp.concatenate([edge_y, after_y[:, :, : plane - layers]], axis=2)
    before_z = low_z(after_z)
    diagonal = coef(reaction) + after_x + before_x + after_y + before_y + after_z + before_z

    def halos(values):
        return (
            forward(values[:, -1:], "gx"),
            backward(values[:, :1], "gx"),
            forward(values[:, :, plane - layers :], "gy"),
            backward(values[:, :, :layers], "gy"),
        )

    def apply_op(values, edges):
        from_low_x, from_high_x, from_low_y, from_high_y = edges
        next_x = jnp.concatenate([values[:, 1:], from_high_x], axis=1)
        prev_x = jnp.concatenate([from_low_x, values[:, :-1]], axis=1)
        next_y = jnp.concatenate([values[:, :, layers:], from_high_y], axis=2)
        prev_y = jnp.concatenate([from_low_y, values[:, :, : plane - layers]], axis=2)
        return (
            diagonal * values
            - after_x * next_x
            - before_x * prev_x
            - after_y * next_y
            - before_y * prev_y
            - after_z * up_z(values)
            - before_z * low_z(values)
        )

    lows = (low_x(after_x), low_y(after_y), before_z)
    ups = (
        up_x(jnp.ones_like(after_x)) * after_x,
        up_y(jnp.ones_like(after_y)) * after_y,
        after_z,
    )
    pivots = diagonal
    for repeat in range(FACT_SWEEPS):
        inv_now = 1.0 / pivots
        pivots = (
            diagonal
            - lows[0] * lows[0] * low_x(inv_now)
            - lows[1] * lows[1] * low_y(inv_now)
            - lows[2] * lows[2] * low_z(inv_now)
        )
    inv_piv = 1.0 / pivots

    def total_gram(former, latter):
        return mesh_sum(block_gram(former, latter))

    def precondition(source):
        lower_sol = inv_piv * source
        for precondition_repeat in range(SWEEPS):
            lower_sol = inv_piv * (
                source
                + lows[0] * low_x(lower_sol)
                + lows[1] * low_y(lower_sol)
                + lows[2] * low_z(lower_sol)
            )
        upper_sol = lower_sol
        for precondition_repeat in range(SWEEPS):
            upper_sol = lower_sol + inv_piv * (
                ups[0] * up_x(upper_sol)
                + ups[1] * up_y(upper_sol)
                + ups[2] * up_z(upper_sol)
            )
        return upper_sol

    start_edges = (
        joint_x[:count_rhs],
        backward(start_in[:, :1], "gx"),
        joint_y[:count_rhs],
        backward(start_in[:, :, :layers], "gy"),
    )
    start_res = rhs_in - apply_op(start_in, start_edges)
    krylov = [start_res]
    precond_set = []
    applied_set = []
    for column in range(ITERS):
        turned = precondition(krylov[-1])
        turned_edges = halos(turned)
        precond_set.append(turned)
        applied_set.append(apply_op(turned, turned_edges))
        krylov.append(applied_set[-1] - SHIFT * krylov[-1])
    leading = jnp.concatenate(krylov[:-1], axis=0)
    leading_gram = block_gram(leading, leading)
    last_cols = block_gram(leading, krylov[-1])
    last_gram = block_gram(krylov[-1], krylov[-1])
    span_gram = mesh_sum(
        jnp.concatenate(
            [
                jnp.concatenate([leading_gram, last_cols], axis=1),
                jnp.concatenate([last_cols.T, last_gram], axis=1),
            ],
            axis=0,
        )
    )
    width = span_gram.shape[0]

    full_low = jnp.linalg.cholesky(span_gram)
    upper = full_low.T
    head = ITERS * count_rhs
    head_inv = lax.linalg.triangular_solve(
        full_low[:head, :head], jnp.eye(head, dtype=jnp.float32), left_side=True, lower=True
    ).T
    advance = jnp.eye(width, head, k=-count_rhs, dtype=jnp.float32) + SHIFT * jnp.eye(width, head, dtype=jnp.float32)
    hessen = jnp.dot(jnp.dot(upper, advance, precision=HIGH), head_inv, precision=HIGH)
    first_factor = upper[:count_rhs, :count_rhs]
    coeffs = solve_small([hessen], first_factor)
    combined = jnp.dot(head_inv, coeffs, precision=HIGH)
    solution = start_in
    residual = start_res
    for column in range(ITERS):
        weights = combined[column * count_rhs : (column + 1) * count_rhs]
        solution = solution + mix_block(precond_set[column], weights)
        residual = residual - mix_block(applied_set[column], weights)
    return (outward(solution), outward(residual))


def solution(mesh):
    return jax.shard_map(
        body,
        mesh=mesh,
        in_specs=(
            P("gx", "gy", None),
            P("gx", "gy", None),
            P("gx", "gy", None),
            P("gx", "gy", None),
            P("gx", "gy", None),
            P("gx", "gy", None),
        ),
        out_specs=(P("gx", "gy", None), P("gx", "gy", None)),
        check_vma=False,
    )
```

```python
import jax
import jax.numpy as jnp
from jax import lax
from jax.sharding import PartitionSpec as P

ITERS = 2
SWEEPS = 4
FACT_SWEEPS = 3
SHIFT = 1.0


HIGH = lax.Precision.HIGHEST


def mesh_sum(block):
    for axis in ("gx", "gy"):
        count = lax.axis_size(axis)
        if count & (count - 1):
            block = lax.psum(block, axis)
            continue
        step = 1
        while step < count:
            radix = 4 if count % (step * 4) == 0 else 2
            parts = [block] + [
                lax.ppermute(block, axis, [(i, i ^ (step * m)) for i in range(count)])
                for m in range(1, radix)
            ]
            while len(parts) > 1:
                parts = [parts[i] + parts[i + 1] for i in range(0, len(parts), 2)]
            block = parts[0]
            step *= radix
    return block


def low_along(values, axis, width):
    count = values.shape[axis]
    blank = jnp.zeros_like(lax.slice_in_dim(values, 0, width, axis=axis))
    return jnp.concatenate([blank, lax.slice_in_dim(values, 0, count - width, axis=axis)], axis=axis)


def up_along(values, axis, width):
    count = values.shape[axis]
    blank = jnp.zeros_like(lax.slice_in_dim(values, 0, width, axis=axis))
    return jnp.concatenate([lax.slice_in_dim(values, width, count, axis=axis), blank], axis=axis)


def block_gram(former, latter):
    return jnp.einsum("sxl,txl->st", former, latter, precision=HIGH)


def mix_block(values, matrix):
    return jnp.einsum("ts,sxl->txl", matrix.T, values, precision=HIGH)


def solve_small(columns, first_factor):
    hessen = jnp.concatenate(columns, axis=1)
    count_rhs = first_factor.shape[0]
    target = jnp.dot(hessen[:count_rhs].T, first_factor, precision=HIGH)
    normal = jnp.dot(hessen.T, hessen, precision=HIGH)
    low_factor = jnp.linalg.cholesky(normal)
    partial_sol = lax.linalg.triangular_solve(low_factor, target, left_side=True, lower=True)
    return lax.linalg.triangular_solve(
        low_factor, partial_sol, left_side=True, lower=True, transpose_a=True
    )


def body(right_side, start_guess, couple_x, couple_y, couple_z, reaction):
    rows_x, rows_y, flat_len = right_side.shape
    layers = couple_z.shape[2]
    count_rhs = flat_len // layers
    plane = rows_y * layers
    depth = jnp.arange(plane, dtype=jnp.int32) % layers
    keep_first = (depth != 0).astype(jnp.float32)
    keep_last = (depth != layers - 1).astype(jnp.float32)

    def inward(values):
        split = values.reshape(rows_x, rows_y, count_rhs, layers)
        return jnp.transpose(split, (2, 0, 1, 3)).reshape(count_rhs, rows_x, plane)

    def outward(values):
        split = values.reshape(count_rhs, rows_x, rows_y, layers)
        return jnp.transpose(split, (1, 2, 0, 3)).reshape(rows_x, rows_y, flat_len)

    def coef(values):
        return values.reshape(1, rows_x, plane)

    def low_x(values):
        return low_along(values, 1, 1)

    def up_x(values):
        return up_along(values, 1, 1)

    def low_y(values):
        return low_along(values, 2, layers)

    def up_y(values):
        return up_along(values, 2, layers)

    def low_z(values):
        return low_along(values, 2, 1) * keep_first

    def up_z(values):
        return up_along(values, 2, 1) * keep_last

    def forward(block, axis):
        count = lax.axis_size(axis)
        return lax.ppermute(block, axis, [(i, i + 1) for i in range(count - 1)])

    def backward(block, axis):
        count = lax.axis_size(axis)
        return lax.ppermute(block, axis, [(i + 1, i) for i in range(count - 1)])

    after_x = coef(couple_x)
    after_y = coef(couple_y)
    after_z = coef(couple_z)
    rhs_in = inward(right_side)
    start_in = inward(start_guess)
    joint_x = forward(jnp.concatenate([start_in[:, -1:], after_x[:, -1:]], axis=0), "gx")
    joint_y = forward(
        jnp.concatenate([start_in[:, :, plane - layers :], after_y[:, :, plane - layers :]], axis=0), "gy"
    )
    edge_x = joint_x[count_rhs:]
    edge_y = joint_y[count_rhs:]
    before_x = jnp.concatenate([edge_x, after_x[:, :-1]], axis=1)
    before_y = jnp.concatenate([edge_y, after_y[:, :, : plane - layers]], axis=2)
    before_z = low_z(after_z)
    diagonal = coef(reaction) + after_x + before_x + after_y + before_y + after_z + before_z

    def halos(values):
        return (
            forward(values[:, -1:], "gx"),
            backward(values[:, :1], "gx"),
            forward(values[:, :, plane - layers :], "gy"),
            backward(values[:, :, :layers], "gy"),
        )

    def apply_op(values, edges):
        from_low_x, from_high_x, from_low_y, from_high_y = edges
        next_x = jnp.concatenate([values[:, 1:], from_high_x], axis=1)
        prev_x = jnp.concatenate([from_low_x, values[:, :-1]], axis=1)
        next_y = jnp.concatenate([values[:, :, layers:], from_high_y], axis=2)
        prev_y = jnp.concatenate([from_low_y, values[:, :, : plane - layers]], axis=2)
        return (
            diagonal * values
            - after_x * next_x
            - before_x * prev_x
            - after_y * next_y
            - before_y * prev_y
            - after_z * up_z(values)
            - before_z * low_z(values)
        )

    lows = (low_x(after_x), low_y(after_y), before_z)
    ups = (
        up_x(jnp.ones_like(after_x)) * after_x,
        up_y(jnp.ones_like(after_y)) * after_y,
        after_z,
    )
    pivots = diagonal
    for repeat in range(FACT_SWEEPS):
        inv_now = 1.0 / pivots
        pivots = (
            diagonal
            - lows[0] * lows[0] * low_x(inv_now)
            - lows[1] * lows[1] * low_y(inv_now)
            - lows[2] * lows[2] * low_z(inv_now)
        )
    inv_piv = 1.0 / pivots
    inv_rev = inv_piv[:, :, ::-1]
    ups_rev = tuple(coupling[:, :, ::-1] for coupling in ups)

    def total_gram(former, latter):
        return mesh_sum(block_gram(former, latter))

    def precondition(source):
        lower_sol = inv_piv * source
        for precondition_repeat in range(SWEEPS):
            lower_sol = inv_piv * (
                source
                + lows[0] * low_x(lower_sol)
                + lows[1] * low_y(lower_sol)
                + lows[2] * low_z(lower_sol)
            )
        lower_rev = lower_sol[:, :, ::-1]
        upper_rev = lower_rev
        for precondition_repeat in range(SWEEPS):
            upper_rev = lower_rev + inv_rev * (
                ups_rev[0] * up_x(upper_rev)
                + ups_rev[1] * low_y(upper_rev)
                + ups_rev[2] * low_z(upper_rev)
            )
        return upper_rev[:, :, ::-1]

    start_edges = (
        joint_x[:count_rhs],
        backward(start_in[:, :1], "gx"),
        joint_y[:count_rhs],
        backward(start_in[:, :, :layers], "gy"),
    )
    start_res = rhs_in - apply_op(start_in, start_edges)
    krylov = [start_res]
    precond_set = []
    applied_set = []
    for column in range(ITERS):
        turned = precondition(krylov[-1])
        turned_edges = halos(turned)
        precond_set.append(turned)
        applied_set.append(apply_op(turned, turned_edges))
        krylov.append(applied_set[-1] - SHIFT * krylov[-1])
    stacked = jnp.concatenate(krylov, axis=0)
    span_gram = mesh_sum(block_gram(stacked, stacked))
    width = span_gram.shape[0]

    full_low = jnp.linalg.cholesky(span_gram)
    upper = full_low.T
    head = ITERS * count_rhs
    head_inv = lax.linalg.triangular_solve(
        full_low[:head, :head], jnp.eye(head, dtype=jnp.float32), left_side=True, lower=True
    ).T
    advance = jnp.eye(width, head, k=-count_rhs, dtype=jnp.float32) + SHIFT * jnp.eye(width, head, dtype=jnp.float32)
    hessen = jnp.dot(jnp.dot(upper, advance, precision=HIGH), head_inv, precision=HIGH)
    first_factor = upper[:count_rhs, :count_rhs]
    coeffs = solve_small([hessen], first_factor)
    combined = jnp.dot(head_inv, coeffs, precision=HIGH)
    solution = start_in
    residual = start_res
    for column in range(ITERS):
        weights = combined[column * count_rhs : (column + 1) * count_rhs]
        solution = solution + mix_block(precond_set[column], weights)
        residual = residual - mix_block(applied_set[column], weights)
    return (outward(solution), outward(residual))


def solution(mesh):
    return jax.shard_map(
        body,
        mesh=mesh,
        in_specs=(
            P("gx", "gy", None),
            P("gx", "gy", None),
            P("gx", "gy", None),
            P("gx", "gy", None),
            P("gx", "gy", None),
            P("gx", "gy", None),
        ),
        out_specs=(P("gx", "gy", None), P("gx", "gy", None)),
        check_vma=False,
    )
```

```python
import jax
import jax.numpy as jnp
from jax import lax
from jax.sharding import PartitionSpec as P

ITERS = 2
SWEEPS = 4
FACT_SWEEPS = 3
SHIFT = 1.0


HIGH = lax.Precision.HIGHEST


def mesh_sum(block):
    for axis in ("gx", "gy"):
        count = lax.axis_size(axis)
        if count & (count - 1):
            block = lax.psum(block, axis)
            continue
        step = 1
        while step < count:
            radix = 4 if count % (step * 4) == 0 else 2
            parts = [block] + [
                lax.ppermute(block, axis, [(i, i ^ (step * m)) for i in range(count)])
                for m in range(1, radix)
            ]
            while len(parts) > 1:
                parts = [parts[i] + parts[i + 1] for i in range(0, len(parts), 2)]
            block = parts[0]
            step *= radix
    return block


def low_along(values, axis, width):
    count = values.shape[axis]
    blank = jnp.zeros_like(lax.slice_in_dim(values, 0, width, axis=axis))
    return jnp.concatenate([blank, lax.slice_in_dim(values, 0, count - width, axis=axis)], axis=axis)


def up_along(values, axis, width):
    count = values.shape[axis]
    blank = jnp.zeros_like(lax.slice_in_dim(values, 0, width, axis=axis))
    return jnp.concatenate([lax.slice_in_dim(values, width, count, axis=axis), blank], axis=axis)


def block_gram(former, latter):
    return jnp.einsum("sxl,txl->st", former, latter, precision=HIGH)


def mix_block(values, matrix):
    return jnp.einsum("ts,sxl->txl", matrix.T, values, precision=HIGH)


def solve_small(columns, first_factor):
    hessen = jnp.concatenate(columns, axis=1)
    count_rhs = first_factor.shape[0]
    target = jnp.dot(hessen[:count_rhs].T, first_factor, precision=HIGH)
    normal = jnp.dot(hessen.T, hessen, precision=HIGH)
    low_factor = lax.linalg.cholesky(normal, symmetrize_input=False)
    partial_sol = lax.linalg.triangular_solve(low_factor, target, left_side=True, lower=True)
    return lax.linalg.triangular_solve(
        low_factor, partial_sol, left_side=True, lower=True, transpose_a=True
    )


def body(right_side, start_guess, couple_x, couple_y, couple_z, reaction):
    rows_x, rows_y, flat_len = right_side.shape
    layers = couple_z.shape[2]
    count_rhs = flat_len // layers
    plane = rows_y * layers
    depth = jnp.arange(plane, dtype=jnp.int32) % layers
    keep_first = (depth != 0).astype(jnp.float32)
    keep_last = (depth != layers - 1).astype(jnp.float32)

    def inward(values):
        split = values.reshape(rows_x, rows_y, count_rhs, layers)
        return jnp.transpose(split, (2, 0, 1, 3)).reshape(count_rhs, rows_x, plane)

    def outward(values):
        split = values.reshape(count_rhs, rows_x, rows_y, layers)
        return jnp.transpose(split, (1, 2, 0, 3)).reshape(rows_x, rows_y, flat_len)

    def coef(values):
        return values.reshape(1, rows_x, plane)

    def low_x(values):
        return low_along(values, 1, 1)

    def up_x(values):
        return up_along(values, 1, 1)

    def low_y(values):
        return low_along(values, 2, layers)

    def up_y(values):
        return up_along(values, 2, layers)

    def low_z(values):
        return low_along(values, 2, 1) * keep_first

    def up_z(values):
        return up_along(values, 2, 1) * keep_last

    def forward(block, axis):
        count = lax.axis_size(axis)
        return lax.ppermute(block, axis, [(i, i + 1) for i in range(count - 1)])

    def backward(block, axis):
        count = lax.axis_size(axis)
        return lax.ppermute(block, axis, [(i + 1, i) for i in range(count - 1)])

    after_x = coef(couple_x)
    after_y = coef(couple_y)
    after_z = coef(couple_z)
    rhs_in = inward(right_side)
    start_in = inward(start_guess)
    joint_x = forward(jnp.concatenate([start_in[:, -1:], after_x[:, -1:]], axis=0), "gx")
    joint_y = forward(
        jnp.concatenate([start_in[:, :, plane - layers :], after_y[:, :, plane - layers :]], axis=0), "gy"
    )
    edge_x = joint_x[count_rhs:]
    edge_y = joint_y[count_rhs:]
    before_x = jnp.concatenate([edge_x, after_x[:, :-1]], axis=1)
    before_y = jnp.concatenate([edge_y, after_y[:, :, : plane - layers]], axis=2)
    before_z = low_z(after_z)
    diagonal = coef(reaction) + after_x + before_x + after_y + before_y + after_z + before_z

    def halos(values):
        return (
            forward(values[:, -1:], "gx"),
            backward(values[:, :1], "gx"),
            forward(values[:, :, plane - layers :], "gy"),
            backward(values[:, :, :layers], "gy"),
        )

    def apply_op(values, edges):
        from_low_x, from_high_x, from_low_y, from_high_y = edges
        next_x = jnp.concatenate([values[:, 1:], from_high_x], axis=1)
        prev_x = jnp.concatenate([from_low_x, values[:, :-1]], axis=1)
        next_y = jnp.concatenate([values[:, :, layers:], from_high_y], axis=2)
        prev_y = jnp.concatenate([from_low_y, values[:, :, : plane - layers]], axis=2)
        return (
            diagonal * values
            - after_x * next_x
            - before_x * prev_x
            - after_y * next_y
            - before_y * prev_y
            - after_z * up_z(values)
            - before_z * low_z(values)
        )

    lows = (low_x(after_x), low_y(after_y), before_z)
    ups = (
        up_x(jnp.ones_like(after_x)) * after_x,
        up_y(jnp.ones_like(after_y)) * after_y,
        after_z,
    )
    pivots = diagonal
    for repeat in range(FACT_SWEEPS):
        inv_now = 1.0 / pivots
        pivots = (
            diagonal
            - lows[0] * lows[0] * low_x(inv_now)
            - lows[1] * lows[1] * low_y(inv_now)
            - lows[2] * lows[2] * low_z(inv_now)
        )
    inv_piv = 1.0 / pivots

    def total_gram(former, latter):
        return mesh_sum(block_gram(former, latter))

    def precondition(source):
        lower_sol = inv_piv * source
        for precondition_repeat in range(SWEEPS):
            lower_sol = inv_piv * (
                source
                + lows[0] * low_x(lower_sol)
                + lows[1] * low_y(lower_sol)
                + lows[2] * low_z(lower_sol)
            )
        upper_sol = lower_sol
        for precondition_repeat in range(SWEEPS):
            upper_sol = lower_sol + inv_piv * (
                ups[0] * up_x(upper_sol)
                + ups[1] * up_y(upper_sol)
                + ups[2] * up_z(upper_sol)
            )
        return upper_sol

    start_edges = (
        joint_x[:count_rhs],
        backward(start_in[:, :1], "gx"),
        joint_y[:count_rhs],
        backward(start_in[:, :, :layers], "gy"),
    )
    start_res = rhs_in - apply_op(start_in, start_edges)
    krylov = [start_res]
    precond_set = []
    applied_set = []
    for column in range(ITERS):
        turned = precondition(krylov[-1])
        turned_edges = halos(turned)
        precond_set.append(turned)
        applied_set.append(apply_op(turned, turned_edges))
        krylov.append(applied_set[-1] - SHIFT * krylov[-1])
    stacked = jnp.concatenate(krylov, axis=0)
    span_gram = mesh_sum(block_gram(stacked, stacked))
    width = span_gram.shape[0]

    full_low = lax.linalg.cholesky(span_gram, symmetrize_input=False)
    upper = full_low.T
    head = ITERS * count_rhs
    head_inv = lax.linalg.triangular_solve(
        full_low[:head, :head], jnp.eye(head, dtype=jnp.float32), left_side=True, lower=True
    ).T
    advance = jnp.eye(width, head, k=-count_rhs, dtype=jnp.float32) + SHIFT * jnp.eye(width, head, dtype=jnp.float32)
    hessen = jnp.dot(jnp.dot(upper, advance, precision=HIGH), head_inv, precision=HIGH)
    first_factor = upper[:count_rhs, :count_rhs]
    coeffs = solve_small([hessen], first_factor)
    combined = jnp.dot(head_inv, coeffs, precision=HIGH)
    solution = start_in
    residual = start_res
    for column in range(ITERS):
        weights = combined[column * count_rhs : (column + 1) * count_rhs]
        solution = solution + mix_block(precond_set[column], weights)
        residual = residual - mix_block(applied_set[column], weights)
    return (outward(solution), outward(residual))


def solution(mesh):
    return jax.shard_map(
        body,
        mesh=mesh,
        in_specs=(
            P("gx", "gy", None),
            P("gx", "gy", None),
            P("gx", "gy", None),
            P("gx", "gy", None),
            P("gx", "gy", None),
            P("gx", "gy", None),
        ),
        out_specs=(P("gx", "gy", None), P("gx", "gy", None)),
        check_vma=False,
    )
```

```python
import jax
import jax.numpy as jnp
from jax import lax
from jax.sharding import PartitionSpec as P

ITERS = 2
SWEEPS = 4
FACT_SWEEPS = 3
SHIFT = 1.0


HIGH = lax.Precision.HIGHEST


def mesh_sum(block):
    for axis in ("gx", "gy"):
        count = lax.axis_size(axis)
        if count & (count - 1):
            block = lax.psum(block, axis)
            continue
        step = 1
        while step < count:
            radix = 4 if count % (step * 4) == 0 else 2
            parts = [block] + [
                lax.ppermute(block, axis, [(i, i ^ (step * m)) for i in range(count)])
                for m in range(1, radix)
            ]
            while len(parts) > 1:
                parts = [parts[i] + parts[i + 1] for i in range(0, len(parts), 2)]
            block = parts[0]
            step *= radix
    return block


def low_along(values, axis, width):
    count = values.shape[axis]
    blank = jnp.zeros_like(lax.slice_in_dim(values, 0, width, axis=axis))
    return jnp.concatenate([blank, lax.slice_in_dim(values, 0, count - width, axis=axis)], axis=axis)


def up_along(values, axis, width):
    config = [(0, 0, 0)] * values.ndim
    config[axis] = (-width, width, 0)
    return lax.pad(values, jnp.zeros((), values.dtype), config)


def block_gram(former, latter):
    return jnp.einsum("sxl,txl->st", former, latter, precision=HIGH)


def mix_block(values, matrix):
    return jnp.einsum("ts,sxl->txl", matrix.T, values, precision=HIGH)


def solve_small(columns, first_factor):
    hessen = jnp.concatenate(columns, axis=1)
    count_rhs = first_factor.shape[0]
    target = jnp.dot(hessen[:count_rhs].T, first_factor, precision=HIGH)
    normal = jnp.dot(hessen.T, hessen, precision=HIGH)
    low_factor = jnp.linalg.cholesky(normal)
    partial_sol = lax.linalg.triangular_solve(low_factor, target, left_side=True, lower=True)
    return lax.linalg.triangular_solve(
        low_factor, partial_sol, left_side=True, lower=True, transpose_a=True
    )


def body(right_side, start_guess, couple_x, couple_y, couple_z, reaction):
    rows_x, rows_y, flat_len = right_side.shape
    layers = couple_z.shape[2]
    count_rhs = flat_len // layers
    plane = rows_y * layers
    depth = jnp.arange(plane, dtype=jnp.int32) % layers
    keep_first = (depth != 0).astype(jnp.float32)
    keep_last = (depth != layers - 1).astype(jnp.float32)

    def inward(values):
        split = values.reshape(rows_x, rows_y, count_rhs, layers)
        return jnp.transpose(split, (2, 0, 1, 3)).reshape(count_rhs, rows_x, plane)

    def outward(values):
        split = values.reshape(count_rhs, rows_x, rows_y, layers)
        return jnp.transpose(split, (1, 2, 0, 3)).reshape(rows_x, rows_y, flat_len)

    def coef(values):
        return values.reshape(1, rows_x, plane)

    def low_x(values):
        return low_along(values, 1, 1)

    def up_x(values):
        return up_along(values, 1, 1)

    def low_y(values):
        return low_along(values, 2, layers)

    def up_y(values):
        return up_along(values, 2, layers)

    def low_z(values):
        return low_along(values, 2, 1) * keep_first

    def up_z(values):
        return up_along(values, 2, 1) * keep_last

    def forward(block, axis):
        count = lax.axis_size(axis)
        return lax.ppermute(block, axis, [(i, i + 1) for i in range(count - 1)])

    def backward(block, axis):
        count = lax.axis_size(axis)
        return lax.ppermute(block, axis, [(i + 1, i) for i in range(count - 1)])

    after_x = coef(couple_x)
    after_y = coef(couple_y)
    after_z = coef(couple_z)
    rhs_in = inward(right_side)
    start_in = inward(start_guess)
    joint_x = forward(jnp.concatenate([start_in[:, -1:], after_x[:, -1:]], axis=0), "gx")
    joint_y = forward(
        jnp.concatenate([start_in[:, :, plane - layers :], after_y[:, :, plane - layers :]], axis=0), "gy"
    )
    edge_x = joint_x[count_rhs:]
    edge_y = joint_y[count_rhs:]
    before_x = jnp.concatenate([edge_x, after_x[:, :-1]], axis=1)
    before_y = jnp.concatenate([edge_y, after_y[:, :, : plane - layers]], axis=2)
    before_z = low_z(after_z)
    diagonal = coef(reaction) + after_x + before_x + after_y + before_y + after_z + before_z

    def halos(values):
        return (
            forward(values[:, -1:], "gx"),
            backward(values[:, :1], "gx"),
            forward(values[:, :, plane - layers :], "gy"),
            backward(values[:, :, :layers], "gy"),
        )

    def apply_op(values, edges):
        from_low_x, from_high_x, from_low_y, from_high_y = edges
        next_x = jnp.concatenate([values[:, 1:], from_high_x], axis=1)
        prev_x = jnp.concatenate([from_low_x, values[:, :-1]], axis=1)
        next_y = jnp.concatenate([values[:, :, layers:], from_high_y], axis=2)
        prev_y = jnp.concatenate([from_low_y, values[:, :, : plane - layers]], axis=2)
        return (
            diagonal * values
            - after_x * next_x
            - before_x * prev_x
            - after_y * next_y
            - before_y * prev_y
            - after_z * up_z(values)
            - before_z * low_z(values)
        )

    lows = (low_x(after_x), low_y(after_y), before_z)
    ups = (
        up_x(jnp.ones_like(after_x)) * after_x,
        up_y(jnp.ones_like(after_y)) * after_y,
        after_z,
    )
    pivots = diagonal
    for repeat in range(FACT_SWEEPS):
        inv_now = 1.0 / pivots
        pivots = (
            diagonal
            - lows[0] * lows[0] * low_x(inv_now)
            - lows[1] * lows[1] * low_y(inv_now)
            - lows[2] * lows[2] * low_z(inv_now)
        )
    inv_piv = 1.0 / pivots

    def total_gram(former, latter):
        return mesh_sum(block_gram(former, latter))

    def precondition(source):
        lower_sol = inv_piv * source
        for precondition_repeat in range(SWEEPS):
            lower_sol = inv_piv * (
                source
                + lows[0] * low_x(lower_sol)
                + lows[1] * low_y(lower_sol)
                + lows[2] * low_z(lower_sol)
            )
        upper_sol = lower_sol
        for precondition_repeat in range(SWEEPS):
            upper_sol = lower_sol + inv_piv * (
                ups[0] * up_x(upper_sol)
                + ups[1] * up_y(upper_sol)
                + ups[2] * up_z(upper_sol)
            )
        return upper_sol

    start_edges = (
        joint_x[:count_rhs],
        backward(start_in[:, :1], "gx"),
        joint_y[:count_rhs],
        backward(start_in[:, :, :layers], "gy"),
    )
    start_res = rhs_in - apply_op(start_in, start_edges)
    krylov = [start_res]
    precond_set = []
    applied_set = []
    for column in range(ITERS):
        turned = precondition(krylov[-1])
        turned_edges = halos(turned)
        precond_set.append(turned)
        applied_set.append(apply_op(turned, turned_edges))
        krylov.append(applied_set[-1] - SHIFT * krylov[-1])
    stacked = jnp.concatenate(krylov, axis=0)
    span_gram = mesh_sum(block_gram(stacked, stacked))
    width = span_gram.shape[0]

    full_low = jnp.linalg.cholesky(span_gram)
    upper = full_low.T
    head = ITERS * count_rhs
    head_inv = lax.linalg.triangular_solve(
        full_low[:head, :head], jnp.eye(head, dtype=jnp.float32), left_side=True, lower=True
    ).T
    advance = jnp.eye(width, head, k=-count_rhs, dtype=jnp.float32) + SHIFT * jnp.eye(width, head, dtype=jnp.float32)
    hessen = jnp.dot(jnp.dot(upper, advance, precision=HIGH), head_inv, precision=HIGH)
    first_factor = upper[:count_rhs, :count_rhs]
    coeffs = solve_small([hessen], first_factor)
    combined = jnp.dot(head_inv, coeffs, precision=HIGH)
    solution = start_in
    residual = start_res
    for column in range(ITERS):
        weights = combined[column * count_rhs : (column + 1) * count_rhs]
        solution = solution + mix_block(precond_set[column], weights)
        residual = residual - mix_block(applied_set[column], weights)
    return (outward(solution), outward(residual))


def solution(mesh):
    return jax.shard_map(
        body,
        mesh=mesh,
        in_specs=(
            P("gx", "gy", None),
            P("gx", "gy", None),
            P("gx", "gy", None),
            P("gx", "gy", None),
            P("gx", "gy", None),
            P("gx", "gy", None),
        ),
        out_specs=(P("gx", "gy", None), P("gx", "gy", None)),
        check_vma=False,
    )
```

```python
import jax
import jax.numpy as jnp
from jax import lax
from jax.sharding import PartitionSpec as P

ITERS = 2
SWEEPS = 4
FACT_SWEEPS = 3
SHIFT = 1.0


HIGH = lax.Precision.HIGHEST


def mesh_sum(block):
    for axis in ("gx", "gy"):
        count = lax.axis_size(axis)
        if count & (count - 1):
            block = lax.psum(block, axis)
            continue
        step = 1
        while step < count:
            radix = 4 if count % (step * 4) == 0 else 2
            parts = [block] + [
                lax.ppermute(block, axis, [(i, i ^ (step * m)) for i in range(count)])
                for m in range(1, radix)
            ]
            while len(parts) > 1:
                parts = [parts[i] + parts[i + 1] for i in range(0, len(parts), 2)]
            block = parts[0]
            step *= radix
    return block


def low_along(values, axis, width):
    config = [(0, 0, 0)] * values.ndim
    config[axis] = (width, -width, 0)
    return lax.pad(values, jnp.zeros((), values.dtype), config)


def up_along(values, axis, width):
    config = [(0, 0, 0)] * values.ndim
    config[axis] = (-width, width, 0)
    return lax.pad(values, jnp.zeros((), values.dtype), config)


def block_gram(former, latter):
    return jnp.einsum("sxl,txl->st", former, latter, precision=HIGH)


def mix_block(values, matrix):
    return jnp.einsum("ts,sxl->txl", matrix.T, values, precision=HIGH)


def solve_small(columns, first_factor):
    hessen = jnp.concatenate(columns, axis=1)
    count_rhs = first_factor.shape[0]
    target = jnp.dot(hessen[:count_rhs].T, first_factor, precision=HIGH)
    normal = jnp.dot(hessen.T, hessen, precision=HIGH)
    low_factor = jnp.linalg.cholesky(normal)
    partial_sol = lax.linalg.triangular_solve(low_factor, target, left_side=True, lower=True)
    return lax.linalg.triangular_solve(
        low_factor, partial_sol, left_side=True, lower=True, transpose_a=True
    )


def body(right_side, start_guess, couple_x, couple_y, couple_z, reaction):
    rows_x, rows_y, flat_len = right_side.shape
    layers = couple_z.shape[2]
    count_rhs = flat_len // layers
    plane = rows_y * layers
    depth = jnp.arange(plane, dtype=jnp.int32) % layers
    keep_first = (depth != 0).astype(jnp.float32)
    keep_last = (depth != layers - 1).astype(jnp.float32)

    def inward(values):
        split = values.reshape(rows_x, rows_y, count_rhs, layers)
        return jnp.transpose(split, (2, 0, 1, 3)).reshape(count_rhs, rows_x, plane)

    def outward(values):
        split = values.reshape(count_rhs, rows_x, rows_y, layers)
        return jnp.transpose(split, (1, 2, 0, 3)).reshape(rows_x, rows_y, flat_len)

    def coef(values):
        return values.reshape(1, rows_x, plane)

    def low_x(values):
        return low_along(values, 1, 1)

    def up_x(values):
        return up_along(values, 1, 1)

    def low_y(values):
        return low_along(values, 2, layers)

    def up_y(values):
        return up_along(values, 2, layers)

    def low_z(values):
        return low_along(values, 2, 1) * keep_first

    def up_z(values):
        return up_along(values, 2, 1) * keep_last

    def forward(block, axis):
        count = lax.axis_size(axis)
        return lax.ppermute(block, axis, [(i, i + 1) for i in range(count - 1)])

    def backward(block, axis):
        count = lax.axis_size(axis)
        return lax.ppermute(block, axis, [(i + 1, i) for i in range(count - 1)])

    after_x = coef(couple_x)
    after_y = coef(couple_y)
    after_z = coef(couple_z)
    rhs_in = inward(right_side)
    start_in = inward(start_guess)
    joint_x = forward(jnp.concatenate([start_in[:, -1:], after_x[:, -1:]], axis=0), "gx")
    joint_y = forward(
        jnp.concatenate([start_in[:, :, plane - layers :], after_y[:, :, plane - layers :]], axis=0), "gy"
    )
    edge_x = joint_x[count_rhs:]
    edge_y = joint_y[count_rhs:]
    before_x = jnp.concatenate([edge_x, after_x[:, :-1]], axis=1)
    before_y = jnp.concatenate([edge_y, after_y[:, :, : plane - layers]], axis=2)
    before_z = low_z(after_z)
    diagonal = coef(reaction) + after_x + before_x + after_y + before_y + after_z + before_z

    def halos(values):
        return (
            forward(values[:, -1:], "gx"),
            backward(values[:, :1], "gx"),
            forward(values[:, :, plane - layers :], "gy"),
            backward(values[:, :, :layers], "gy"),
        )

    def apply_op(values, edges):
        from_low_x, from_high_x, from_low_y, from_high_y = edges
        next_x = jnp.concatenate([values[:, 1:], from_high_x], axis=1)
        prev_x = jnp.concatenate([from_low_x, values[:, :-1]], axis=1)
        next_y = jnp.concatenate([values[:, :, layers:], from_high_y], axis=2)
        prev_y = jnp.concatenate([from_low_y, values[:, :, : plane - layers]], axis=2)
        return (
            diagonal * values
            - after_x * next_x
            - before_x * prev_x
            - after_y * next_y
            - before_y * prev_y
            - after_z * up_z(values)
            - before_z * low_z(values)
        )

    lows = (low_x(after_x), low_y(after_y), before_z)
    ups = (
        up_x(jnp.ones_like(after_x)) * after_x,
        up_y(jnp.ones_like(after_y)) * after_y,
        after_z,
    )
    pivots = diagonal
    for repeat in range(FACT_SWEEPS):
        inv_now = 1.0 / pivots
        pivots = (
            diagonal
            - lows[0] * lows[0] * low_x(inv_now)
            - lows[1] * lows[1] * low_y(inv_now)
            - lows[2] * lows[2] * low_z(inv_now)
        )
    inv_piv = 1.0 / pivots

    def total_gram(former, latter):
        return mesh_sum(block_gram(former, latter))

    def precondition(source):
        lower_sol = inv_piv * source
        for precondition_repeat in range(SWEEPS):
            lower_sol = inv_piv * (
                source
                + lows[0] * low_x(lower_sol)
                + lows[1] * low_y(lower_sol)
                + lows[2] * low_z(lower_sol)
            )
        upper_sol = lower_sol
        for precondition_repeat in range(SWEEPS):
            upper_sol = lower_sol + inv_piv * (
                ups[0] * up_x(upper_sol)
                + ups[1] * up_y(upper_sol)
                + ups[2] * up_z(upper_sol)
            )
        return upper_sol

    start_edges = (
        joint_x[:count_rhs],
        backward(start_in[:, :1], "gx"),
        joint_y[:count_rhs],
        backward(start_in[:, :, :layers], "gy"),
    )
    start_res = rhs_in - apply_op(start_in, start_edges)
    krylov = [start_res]
    precond_set = []
    applied_set = []
    for column in range(ITERS):
        turned = precondition(krylov[-1])
        turned_edges = halos(turned)
        precond_set.append(turned)
        applied_set.append(apply_op(turned, turned_edges))
        krylov.append(applied_set[-1] - SHIFT * krylov[-1])
    stacked = jnp.concatenate(krylov, axis=0)
    span_gram = mesh_sum(block_gram(stacked, stacked))
    width = span_gram.shape[0]

    full_low = jnp.linalg.cholesky(span_gram)
    upper = full_low.T
    head = ITERS * count_rhs
    head_inv = lax.linalg.triangular_solve(
        full_low[:head, :head], jnp.eye(head, dtype=jnp.float32), left_side=True, lower=True
    ).T
    advance = jnp.eye(width, head, k=-count_rhs, dtype=jnp.float32) + SHIFT * jnp.eye(width, head, dtype=jnp.float32)
    hessen = jnp.dot(jnp.dot(upper, advance, precision=HIGH), head_inv, precision=HIGH)
    first_factor = upper[:count_rhs, :count_rhs]
    coeffs = solve_small([hessen], first_factor)
    combined = jnp.dot(head_inv, coeffs, precision=HIGH)
    solution = start_in
    residual = start_res
    for column in range(ITERS):
        weights = combined[column * count_rhs : (column + 1) * count_rhs]
        solution = solution + mix_block(precond_set[column], weights)
        residual = residual - mix_block(applied_set[column], weights)
    return (outward(solution), outward(residual))


def solution(mesh):
    return jax.shard_map(
        body,
        mesh=mesh,
        in_specs=(
            P("gx", "gy", None),
            P("gx", "gy", None),
            P("gx", "gy", None),
            P("gx", "gy", None),
            P("gx", "gy", None),
            P("gx", "gy", None),
        ),
        out_specs=(P("gx", "gy", None), P("gx", "gy", None)),
        check_vma=False,
    )
```
